32 devices in a mesh: member: 2 (over x), row: 16 (over z, y, core).
Axes of the slice: x: 2, y: 2, z: 4, core: 2. Of those that a mesh axis runs over, the one named last changes fastest.
Arguments:
- coarse: bfloat16 [384, 128, 128], P('row', 'member'), parts along dimension 1, may hold values from -6 to 6
- skip_field: bfloat16 [192, 256, 256], P(None, ('member', 'row')), parts along dimension 1, may hold values from -6 to 6
- up_weight: bfloat16 [4, 4, 384, 192], replicated, may hold values from -0.15625 to 0.15625
- up_bias: float32 [192], replicated, may hold values from -3 to 3
- conv_weight: bfloat16 [3, 3, 384, 192], replicated, may hold values from -0.109375 to 0.109375
- conv_bias: float32 [192], replicated, may hold values from -3 to 3
Outputs:
- decoded: bfloat16 [192, 256, 256], P(None, ('member', 'row')), parts along dimension 1
The draws below stay inside these ranges and needn't reach their ends.
There are 2 independent parts, one for each index of `member`. The reference program is written for one: setup_inputs(seed, part) draws one part's arguments, and reference() takes and returns one part's arrays. A program takes and returns all parts, laid end to end along the dimension named above; an argument that names none is the same for every part. Nothing has to cross between parts.
All inputs are finite; a program needn't handle non-finite values.
Results may differ from the reference program's by a relative error of at most 0.0055.
Values may be sent and summed in bfloat16 or wider, within the bound.
No kernel may reach another device: no remote copies, remote signals or barrier semaphores. Data moves between devices by JAX's collectives and lax.ppermute only.
A program may use at most 64 MiB of HBM per device.

```python
import jax
import jax.numpy as jnp

CIN = 384
COUT = 192
FW = 256
FH = 128
CH = 64
CW = 128


def levels(stream_key, shape, split, least, high):
    gain, own = 1.0, jax.random.fold_in(stream_key, 6)
    for dim, blocks in split:
        steps = jnp.exp(jax.random.uniform(jax.random.fold_in(own, dim), (blocks,), jnp.float32, least / len(split), high / len(split)))
        gain = gain * jnp.repeat(steps, shape[dim] // blocks).reshape([-1 if axis == dim else 1 for axis in range(len(shape))])
    return gain


def scatter_about(key, extent, spread, reach, cuts=(), dtype=jnp.bfloat16):
    drawn = spread * jax.random.normal(key, extent, jnp.float32)
    if cuts:
        drawn = drawn * levels(key, extent, cuts, -0.22, 0.18)
    return jnp.clip(drawn, -reach, reach).astype(dtype)


def setup_inputs(seed: int = 0, part: int = 0) -> dict:
    arg_keys = jax.random.split(jax.random.key(seed), 7)
    part_splits = jax.random.split(jax.random.fold_in(arg_keys[6], part), 7)
    return {
        "coarse": scatter_about(part_splits[0], (CIN, CH, CW), 1.0, 6.0, ((0, 16),)),
        "skip_field": scatter_about(part_splits[1], (COUT, FH, FW), 1.0, 6.0, ((1, 16),)),
        "up_weight": scatter_about(arg_keys[2], (4, 4, CIN, COUT), (4 * CIN) ** -0.5, 0.15625),
        "up_bias": scatter_about(arg_keys[3], (COUT,), 0.5, 3.0, (), jnp.float32),
        "conv_weight": scatter_about(arg_keys[4], (3, 3, 2 * COUT, COUT), (18 * COUT) ** -0.5, 0.109375),
        "conv_bias": scatter_about(arg_keys[5], (COUT,), 0.5, 3.0, (), jnp.float32),
    }


TAP_TABLE = (((0, 3), (1, 1)), ((1, 2), (2, 0)))


def upsample(padded, weight):
    span_rows = padded.shape[1] - 2
    span_cols = padded.shape[2] - 2
    outputs = weight.shape[3]
    row_parts = []
    for row_par in range(2):
        col_parts = []
        for col_par in range(2):
            summed = jnp.zeros((outputs, span_rows, span_cols), jnp.float32)
            for row_off, row_tap in TAP_TABLE[row_par]:
                for col_off, col_tap in TAP_TABLE[col_par]:
                    window = padded[:, row_off:row_off + span_rows, col_off:col_off + span_cols].astype(jnp.float32)
                    summed = summed + jnp.einsum("chw,co->ohw", window, weight[row_tap, col_tap].astype(jnp.float32))
            col_parts.append(summed)
        row_parts.append(jnp.stack(col_parts, axis=-1))
    stacked = jnp.stack(row_parts, axis=2)
    return stacked.reshape(outputs, 2 * span_rows, 2 * span_cols)


def conv_taps(padded, weight):
    span_rows = padded.shape[1] - 2
    span_cols = padded.shape[2] - 2
    summed = jnp.zeros((weight.shape[3], span_rows, span_cols), jnp.float32)
    for row_tap in range(3):
        for col_tap in range(3):
            window = padded[:, row_tap:row_tap + span_rows, col_tap:col_tap + span_cols].astype(jnp.float32)
            summed = summed + jnp.einsum("chw,co->ohw", window, weight[row_tap, col_tap].astype(jnp.float32))
    return summed


def reference(coarse, skip_field, up_weight, up_bias, conv_weight, conv_bias):
    padded = jnp.pad(coarse, ((0, 0), (1, 1), (1, 1)))
    raised = upsample(padded, up_weight) + up_bias[:, None, None]
    upsampled = raised.astype(jnp.bfloat16)
    joined = jnp.concatenate([skip_field, upsampled], axis=0)
    padded_fine = jnp.pad(joined, ((0, 0), (1, 1), (1, 1)))
    pre = conv_taps(padded_fine, conv_weight) + conv_bias[:, None, None]
    return jax.nn.silu(pre).astype(jnp.bfloat16)
```

```python
import jax
import jax.numpy as jnp
from jax import lax
from jax.sharding import PartitionSpec as P

CHW = ("NCHW", "HWIO", "NCHW")


def coarse_windows(coarse, peers):
    groups, rows, cols = coarse.shape
    tile = rows // peers
    padded = jnp.pad(coarse, ((0, 0), (1, tile - 1), (0, 0)))
    blocks = padded.reshape(groups, peers + 1, tile, cols)
    windows = jnp.concatenate([blocks[:, :peers], blocks[:, 1:, :2]], axis=2)
    windows = jnp.transpose(windows, (1, 0, 2, 3))
    gathered = lax.all_to_all(windows, "row", 0, 0, tiled=True)
    return gathered.reshape(peers * groups, tile + 2, cols)


def skip_rim(skip, peers):
    up = [(i, i + 1) for i in range(peers - 1)]
    down = [(j, i) for i, j in up]
    before = lax.ppermute(skip[:, -1:], "row", up)
    after = lax.ppermute(skip[:, :1], "row", down)
    return jnp.concatenate([before, skip, after], axis=1)


def upsample(window, up_weight, up_bias):
    kernel = up_weight[::-1, ::-1]
    raised = lax.conv_general_dilated(
        window[None],
        kernel,
        window_strides=(1, 1),
        padding=((1, 1), (2, 2)),
        lhs_dilation=(2, 2),
        dimension_numbers=CHW,
        preferred_element_type=jnp.float32,
    )[0]
    return raised + up_bias[:, None, None]


def conv3(field, weight):
    return lax.conv_general_dilated(
        field[None],
        weight,
        window_strides=(1, 1),
        padding=((0, 0), (1, 1)),
        dimension_numbers=CHW,
        preferred_element_type=jnp.float32,
    )[0]


def shards(coarse, skip_field, up_weight, up_bias, conv_weight, conv_bias):
    peers = lax.axis_size("row")
    me = lax.axis_index("row")
    skip_ext = skip_rim(skip_field, peers)
    window = coarse_windows(coarse, peers)
    raised = upsample(window, up_weight, up_bias)
    fine = raised.shape[1]
    row = lax.broadcasted_iota(jnp.int32, (1, fine, 1), 1)
    outside = ((row == 0) & (me == 0)) | ((row == fine - 1) & (me == peers - 1))
    upsampled = jnp.where(outside, 0.0, raised).astype(jnp.bfloat16)
    skips = skip_field.shape[0]
    pre = conv3(skip_ext, conv_weight[:, :, :skips]) + conv3(upsampled, conv_weight[:, :, skips:])
    pre = pre + conv_bias[:, None, None]
    return jax.nn.silu(pre).astype(jnp.bfloat16)


def solution(mesh):
    in_specs = (P("row", "member", None), P(None, ("member", "row"), None), P(), P(), P(), P())
    out_specs = P(None, ("member", "row"), None)
    return jax.shard_map(shards, mesh=mesh, in_specs=in_specs, out_specs=out_specs, check_vma=False)
```

```python
import jax
import jax.numpy as jnp
from jax import lax
from jax.experimental import pallas as pl
from jax.experimental.pallas import tpu as pltpu
from jax.sharding import PartitionSpec as P


def coarse_windows(coarse, peers):
    groups, rows, cols = coarse.shape
    tile = rows // peers
    padded = jnp.pad(coarse, ((0, 0), (1, tile - 1), (0, 0)))
    blocks = padded.reshape(groups, peers + 1, tile, cols)
    windows = jnp.concatenate([blocks[:, :peers], blocks[:, 1:, :2]], axis=2)
    windows = jnp.transpose(windows, (1, 2, 0, 3))
    gathered = lax.all_to_all(windows, "row", 0, 2, tiled=True)
    return gathered.reshape(tile + 2, peers * groups, cols)


def skip_rows(skip, peers):
    up = [(i, i + 1) for i in range(peers - 1)]
    down = [(j, i) for i, j in up]
    before = lax.ppermute(skip[:, -1:], "row", up)
    after = lax.ppermute(skip[:, :1], "row", down)
    rimmed = jnp.concatenate([before, skip, after], axis=1)
    return jnp.transpose(rimmed, (1, 0, 2))


def lane_shift(v, period, step):
    lane = lax.broadcasted_iota(jnp.int32, v.shape, 1) % period
    edge = 0 if step > 0 else period - 1
    return jnp.where(lane == edge, 0.0, pltpu.roll(v, step % v.shape[1], 1))


def decoder_kernel(flags, xw_ref, sk_ref, wu_ref, bu_ref, w3_ref, b3_ref, out_ref):
    nwin, cin, cw = xw_ref.shape
    nfine, cout, fw = sk_ref.shape
    nout = nfine - 2
    span = (nwin - 1) * cw
    f32 = jnp.float32

    def dot(a, b):
        return jnp.dot(a, b, preferred_element_type=f32)

    wide = jnp.concatenate([xw_ref[i] for i in range(nwin)], axis=1)
    later, earlier = wide[:, cw:], wide[:, :span]
    parity = []
    for first, second in ((0, 2), (1, 3)):
        z = dot(wu_ref[first], later) + dot(wu_ref[second], earlier)
        taps = [z[k * cout : (k + 1) * cout] for k in range(4)]
        even = taps[1] + lane_shift(taps[3], cw, 1) + bu_ref[...]
        odd = taps[2] + lane_shift(taps[0], cw, -1) + bu_ref[...]
        parity.append((even.astype(jnp.bfloat16), odd.astype(jnp.bfloat16)))

    col = lax.broadcasted_iota(jnp.int32, (cw, fw), 0)
    pos = lax.broadcasted_iota(jnp.int32, (cw, fw), 1)
    put_even = (pos == 2 * col).astype(jnp.bfloat16)
    put_odd = (pos == 2 * col + 1).astype(jnp.bfloat16)

    joined = []
    for t in range(nfine):
        even, odd = parity[t % 2]
        q = t // 2
        row = dot(even[:, q * cw : (q + 1) * cw], put_even) + dot(odd[:, q * cw : (q + 1) * cw], put_odd)
        if t == 0:
            row = jnp.where(flags[0] == 1, 0.0, row)
        if t == nfine - 1:
            row = jnp.where(flags[1] == 1, 0.0, row)
        joined.append(jnp.concatenate([sk_ref[t], row.astype(jnp.bfloat16)], axis=0))
    field = jnp.concatenate(joined, axis=1)

    total = None
    for ky in range(3):
        part = dot(w3_ref[ky], field[:, ky * fw : (ky + nout) * fw])
        total = part if total is None else total + part
    pre = total[cout : 2 * cout]
    pre = pre + lane_shift(total[:cout], fw, 1) + lane_shift(total[2 * cout :], fw, -1)
    pre = pre + b3_ref[...]
    act = (pre / (1.0 + jnp.exp(-pre))).astype(out_ref.dtype)
    for y in range(nout):
        out_ref[y] = act[:, y * fw : (y + 1) * fw]


def decode(flags, xw, sk, wu, bu, w3, b3):
    nfine, cout, fw = sk.shape
    vmem = pl.BlockSpec(memory_space=pltpu.VMEM)
    return pl.pallas_call(
        decoder_kernel,
        out_shape=jax.ShapeDtypeStruct((nfine - 2, cout, fw), jnp.bfloat16),
        in_specs=[pl.BlockSpec(memory_space=pltpu.SMEM)] + [vmem] * 6,
        out_specs=vmem,
        compiler_params=pltpu.CompilerParams(vmem_limit_bytes=48 * 1024 * 1024),
    )(flags, xw, sk, wu, bu, w3, b3)


def shards(coarse, skip_field, up_weight, up_bias, conv_weight, conv_bias):
    peers = lax.axis_size("row")
    me = lax.axis_index("row")
    flags = jnp.stack([me == 0, me == peers - 1]).astype(jnp.int32)
    sk = skip_rows(skip_field, peers)
    xw = coarse_windows(coarse, peers)
    cout = up_weight.shape[3]
    wu = jnp.transpose(up_weight, (0, 1, 3, 2)).reshape(4, 4 * cout, -1)
    w3 = jnp.transpose(conv_weight, (0, 1, 3, 2)).reshape(3, 3 * cout, -1)
    out = decode(flags, xw, sk, wu, up_bias[:, None], w3, conv_bias[:, None])
    return jnp.transpose(out, (1, 0, 2))


def solution(mesh):
    in_specs = (P("row", "member", None), P(None, ("member", "row"), None), P(), P(), P(), P())
    out_specs = P(None, ("member", "row"), None)
    return jax.shard_map(shards, mesh=mesh, in_specs=in_specs, out_specs=out_specs, check_vma=False)
```

```python
import jax
import jax.numpy as jnp
from jax import lax
from jax.experimental import pallas as pl
from jax.experimental.pallas import tpu as pltpu
from jax.sharding import PartitionSpec as P


def coarse_windows(coarse, peers):
    groups, rows, cols = coarse.shape
    tile = rows // peers
    padded = jnp.pad(coarse, ((0, 0), (1, tile - 1), (0, 0)))
    blocks = padded.reshape(groups, peers + 1, tile, cols)
    windows = jnp.concatenate([blocks[:, :peers], blocks[:, 1:, :2]], axis=2)
    windows = jnp.transpose(windows, (1, 2, 0, 3))
    gathered = lax.all_to_all(windows, "row", 0, 2, tiled=True)
    return gathered.reshape(tile + 2, peers * groups, cols)


def skip_rows(skip, peers):
    up = [(i, i + 1) for i in range(peers - 1)]
    down = [(j, i) for i, j in up]
    before = lax.ppermute(skip[:, -1:], "row", up)
    after = lax.ppermute(skip[:, :1], "row", down)
    rimmed = jnp.concatenate([before, skip, after], axis=1)
    return jnp.transpose(rimmed, (1, 0, 2))


def lane_shift(v, period, step):
    lane = lax.broadcasted_iota(jnp.int32, v.shape, 1) % period
    edge = 0 if step > 0 else period - 1
    return jnp.where(lane == edge, 0.0, pltpu.roll(v, step % v.shape[1], 1))


def conv_rows(field, w_ref, nout, fw):
    total = None
    for ky in range(3):
        part = jnp.dot(w_ref[ky], field[:, ky * fw : (ky + nout) * fw], preferred_element_type=jnp.float32)
        total = part if total is None else total + part
    cout = total.shape[0] // 3
    mid = total[cout : 2 * cout]
    return mid + lane_shift(total[:cout], fw, 1) + lane_shift(total[2 * cout :], fw, -1)


def skip_kernel(sk_ref, w_ref, b_ref, out_ref):
    nfine, _, fw = sk_ref.shape
    field = jnp.concatenate([sk_ref[t] for t in range(nfine)], axis=1)
    out_ref[...] = conv_rows(field, w_ref, nfine - 2, fw) + b_ref[...]


def decoder_kernel(flags, xw_ref, wu_ref, bu_ref, w3_ref, part_ref, out_ref):
    nwin, cin, cw = xw_ref.shape
    cout, nout, fw = out_ref.shape
    nfine = nout + 2
    span = (nwin - 1) * cw
    f32 = jnp.float32

    def dot(a, b):
        return jnp.dot(a, b, preferred_element_type=f32)

    wide = jnp.concatenate([xw_ref[i] for i in range(nwin)], axis=1)
    later, earlier = wide[:, cw:], wide[:, :span]
    parity = []
    for first, second in ((0, 2), (1, 3)):
        z = dot(wu_ref[first], later) + dot(wu_ref[second], earlier)
        taps = [z[k * cout : (k + 1) * cout] for k in range(4)]
        even = taps[1] + lane_shift(taps[3], cw, 1) + bu_ref[...]
        odd = taps[2] + lane_shift(taps[0], cw, -1) + bu_ref[...]
        parity.append((even.astype(jnp.bfloat16), odd.astype(jnp.bfloat16)))

    col = lax.broadcasted_iota(jnp.int32, (cw, fw), 0)
    pos = lax.broadcasted_iota(jnp.int32, (cw, fw), 1)
    put_even = (pos == 2 * col).astype(jnp.bfloat16)
    put_odd = (pos == 2 * col + 1).astype(jnp.bfloat16)

    rows = []
    for t in range(nfine):
        even, odd = parity[t % 2]
        q = t // 2
        row = dot(even[:, q * cw : (q + 1) * cw], put_even) + dot(odd[:, q * cw : (q + 1) * cw], put_odd)
        if t == 0:
            row = jnp.where(flags[0] == 1, 0.0, row)
        if t == nfine - 1:
            row = jnp.where(flags[1] == 1, 0.0, row)
        rows.append(row.astype(jnp.bfloat16))
    field = jnp.concatenate(rows, axis=1)

    pre = conv_rows(field, w3_ref, nout, fw) + part_ref[...]
    act = (pre / (1.0 + jnp.exp(-pre))).astype(out_ref.dtype)
    for y in range(nout):
        out_ref[:, y, :] = act[:, y * fw : (y + 1) * fw]


def skip_conv(sk, w3s, b3):
    nfine, cout, fw = sk.shape
    nout = nfine - 2
    vmem = pl.BlockSpec(memory_space=pltpu.VMEM)
    flops = 2 * 3 * w3s.shape[1] * w3s.shape[2] * nout * fw
    return pl.pallas_call(
        skip_kernel,
        out_shape=jax.ShapeDtypeStruct((cout, nout * fw), jnp.float32),
        in_specs=[vmem] * 3,
        out_specs=vmem,
        compiler_params=pltpu.CompilerParams(vmem_limit_bytes=48 * 1024 * 1024),
        cost_estimate=pl.CostEstimate(flops=flops, transcendentals=0, bytes_accessed=sk.size * 2 + w3s.size * 2 + cout * nout * fw * 4),
    )(sk, w3s, b3)


def decode(flags, xw, wu, bu, w3u, part, nout, fw):
    cout = bu.shape[0]
    vmem = pl.BlockSpec(memory_space=pltpu.VMEM)
    return pl.pallas_call(
        decoder_kernel,
        out_shape=jax.ShapeDtypeStruct((cout, nout, fw), jnp.bfloat16),
        in_specs=[pl.BlockSpec(memory_space=pltpu.SMEM)] + [vmem] * 5,
        out_specs=vmem,
        compiler_params=pltpu.CompilerParams(vmem_limit_bytes=48 * 1024 * 1024),
    )(flags, xw, wu, bu, w3u, part)


def shards(coarse, skip_field, up_weight, up_bias, conv_weight, conv_bias):
    peers = lax.axis_size("row")
    me = lax.axis_index("row")
    flags = jnp.stack([me == 0, me == peers - 1]).astype(jnp.int32)
    sk = skip_rows(skip_field, peers)
    xw = coarse_windows(coarse, peers)
    cout = up_weight.shape[3]
    wu = jnp.transpose(up_weight, (0, 1, 3, 2)).reshape(4, 4 * cout, -1)
    w3 = jnp.transpose(conv_weight, (0, 1, 3, 2)).reshape(3, 3 * cout, -1)
    skips = skip_field.shape[0]
    part = skip_conv(sk, w3[:, :, :skips], conv_bias[:, None])
    nout, fw = skip_field.shape[1], skip_field.shape[2]
    return decode(flags, xw, wu, up_bias[:, None], w3[:, :, skips:], part, nout, fw)


def solution(mesh):
    in_specs = (P("row", "member", None), P(None, ("member", "row"), None), P(), P(), P(), P())
    out_specs = P(None, ("member", "row"), None)
    return jax.shard_map(shards, mesh=mesh, in_specs=in_specs, out_specs=out_specs, check_vma=False)
```

```python
import jax
import jax.numpy as jnp
from jax import lax
from jax.experimental import pallas as pl
from jax.experimental.pallas import tpu as pltpu
from jax.sharding import PartitionSpec as P


def coarse_windows(coarse, peers):
    groups, rows, cols = coarse.shape
    tile = rows // peers
    padded = jnp.pad(coarse, ((0, 0), (1, 1), (0, 0)))
    windows = jnp.stack([padded[:, r * tile : r * tile + tile + 2] for r in range(peers)])
    windows = jnp.transpose(windows, (0, 2, 1, 3))
    gathered = lax.all_to_all(windows, "row", 0, 0, tiled=True)
    if groups % 8:
        gathered = jnp.transpose(gathered, (1, 0, 2, 3)).reshape(1, tile + 2, peers * groups, cols)
    return gathered


def skip_rows(skip, peers):
    up = [(i, i + 1) for i in range(peers - 1)]
    down = [(j, i) for i, j in up]
    before = lax.ppermute(skip[:, -1:], "row", up)
    after = lax.ppermute(skip[:, :1], "row", down)
    rimmed = jnp.concatenate([before, skip, after], axis=1)
    return jnp.transpose(rimmed, (1, 0, 2))


def lane_shift(v, period, step):
    lane = lax.broadcasted_iota(jnp.int32, v.shape, 1) % period
    edge = 0 if step > 0 else period - 1
    return jnp.where(lane == edge, 0.0, pltpu.roll(v, step % v.shape[1], 1))


def decoder_kernel(flags, xw_ref, sk_ref, wu_ref, bu_ref, w3_ref, b3_ref, out_ref, act_ref):
    peers, nwin, groups, cw = xw_ref.shape
    nfine, cout, fw = sk_ref.shape
    nout = nfine - 2
    span = (nwin - 1) * cw
    f32 = jnp.float32

    def dot(a, b):
        return jnp.dot(a, b, preferred_element_type=f32)

    def window_row(i):
        if peers == 1:
            return xw_ref[0, i]
        pieces = [xw_ref[s, i].astype(f32) for s in range(peers)]
        return jnp.concatenate(pieces, axis=0).astype(jnp.bfloat16)

    wide = jnp.concatenate([window_row(i) for i in range(nwin)], axis=1)
    later, earlier = wide[:, cw:], wide[:, :span]
    parity = []
    for first, second in ((0, 2), (1, 3)):
        z = dot(wu_ref[first], later) + dot(wu_ref[second], earlier)
        taps = [z[k * cout : (k + 1) * cout] for k in range(4)]
        even = taps[1] + lane_shift(taps[3], cw, 1) + bu_ref[...]
        odd = taps[2] + lane_shift(taps[0], cw, -1) + bu_ref[...]
        parity.append((even.astype(jnp.bfloat16), odd.astype(jnp.bfloat16)))

    col = lax.broadcasted_iota(jnp.int32, (cw, fw), 0)
    pos = lax.broadcasted_iota(jnp.int32, (cw, fw), 1)
    put_even = (pos == 2 * col).astype(jnp.bfloat16)
    put_odd = (pos == 2 * col + 1).astype(jnp.bfloat16)

    joined = []
    for t in range(nfine):
        even, odd = parity[t % 2]
        q = t // 2
        row = dot(even[:, q * cw : (q + 1) * cw], put_even) + dot(odd[:, q * cw : (q + 1) * cw], put_odd)
        if t == 0:
            row = jnp.where(flags[0] == 1, 0.0, row)
        if t == nfine - 1:
            row = jnp.where(flags[1] == 1, 0.0, row)
        joined.append(jnp.concatenate([sk_ref[t], row.astype(jnp.bfloat16)], axis=0))
    field = jnp.concatenate(joined, axis=1)

    total = None
    for ky in range(3):
        part = dot(w3_ref[ky], field[:, ky * fw : (ky + nout) * fw])
        total = part if total is None else total + part
    pre = total[cout : 2 * cout]
    pre = pre + lane_shift(total[:cout], fw, 1) + lane_shift(total[2 * cout :], fw, -1)
    pre = pre + b3_ref[...]
    act = pre / (1.0 + jnp.exp(-pre))
    for y in range(nout):
        act_ref[:, y, :] = act[:, y * fw : (y + 1) * fw]
    out_ref[...] = act_ref[...].astype(out_ref.dtype)


def decode(flags, xw, sk, wu, bu, w3, b3):
    nfine, cout, fw = sk.shape
    vmem = pl.BlockSpec(memory_space=pltpu.VMEM)
    return pl.pallas_call(
        decoder_kernel,
        out_shape=jax.ShapeDtypeStruct((cout, nfine - 2, fw), jnp.bfloat16),
        in_specs=[pl.BlockSpec(memory_space=pltpu.SMEM)] + [vmem] * 6,
        out_specs=vmem,
        scratch_shapes=[pltpu.VMEM((cout, nfine - 2, fw), jnp.float32)],
        compiler_params=pltpu.CompilerParams(vmem_limit_bytes=48 * 1024 * 1024),
    )(flags, xw, sk, wu, bu, w3, b3)


def shards(coarse, skip_field, up_weight, up_bias, conv_weight, conv_bias):
    peers = lax.axis_size("row")
    me = lax.axis_index("row")
    flags = jnp.stack([me == 0, me == peers - 1]).astype(jnp.int32)
    sk = skip_rows(skip_field, peers)
    xw = coarse_windows(coarse, peers)
    cout = up_weight.shape[3]
    wu = jnp.transpose(up_weight, (0, 1, 3, 2)).reshape(4, 4 * cout, -1)
    w3 = jnp.transpose(conv_weight, (0, 1, 3, 2)).reshape(3, 3 * cout, -1)
    return decode(flags, xw, sk, wu, up_bias[:, None], w3, conv_bias[:, None])


def solution(mesh):
    in_specs = (P("row", "member", None), P(None, ("member", "row"), None), P(), P(), P(), P())
    out_specs = P(None, ("member", "row"), None)
    return jax.shard_map(shards, mesh=mesh, in_specs=in_specs, out_specs=out_specs, check_vma=False)
```

```python
import jax
import jax.numpy as jnp
from jax import lax
from jax.experimental import pallas as pl
from jax.experimental.pallas import tpu as pltpu
from jax.sharding import PartitionSpec as P


def coarse_windows(coarse, peers):
    groups, rows, cols = coarse.shape
    tile = rows // peers
    padded = jnp.pad(coarse, ((0, 0), (1, tile - 1), (0, 0)))
    blocks = padded.reshape(groups, peers + 1, tile, cols)
    windows = jnp.concatenate([blocks[:, :peers], blocks[:, 1:, :2]], axis=2)
    windows = jnp.transpose(windows, (1, 2, 0, 3))
    gathered = lax.all_to_all(windows, "row", 0, 0, tiled=True)
    if groups % 8:
        gathered = jnp.transpose(gathered, (1, 0, 2, 3)).reshape(1, tile + 2, peers * groups, cols)
    return gathered


def skip_rows(skip, peers):
    up = [(i, i + 1) for i in range(peers - 1)]
    down = [(j, i) for i, j in up]
    before = lax.ppermute(skip[:, -1:], "row", up)
    after = lax.ppermute(skip[:, :1], "row", down)
    rimmed = jnp.concatenate([before, skip, after], axis=1)
    return jnp.transpose(rimmed, (1, 0, 2))


def lane_shift(v, period, step):
    lane = lax.broadcasted_iota(jnp.int32, v.shape, 1) % period
    edge = 0 if step > 0 else period - 1
    return jnp.where(lane == edge, 0.0, pltpu.roll(v, step % v.shape[1], 1))


def decoder_kernel(flags, xw_ref, sk_ref, wu_ref, bu_ref, w3_ref, b3_ref, out_ref, act_ref):
    peers, nwin, groups, cw = xw_ref.shape
    nfine, cout, fw = sk_ref.shape
    nout = nfine - 2
    span = (nwin - 1) * cw
    f32 = jnp.float32

    def dot(a, b):
        return jnp.dot(a, b, preferred_element_type=f32)

    def window_row(i):
        if peers == 1:
            return xw_ref[0, i]
        pieces = [xw_ref[s, i].astype(f32) for s in range(peers)]
        return jnp.concatenate(pieces, axis=0).astype(jnp.bfloat16)

    wide = jnp.concatenate([window_row(i) for i in range(nwin)], axis=1)
    later, earlier = wide[:, cw:], wide[:, :span]
    parity = []
    for first, second in ((0, 2), (1, 3)):
        z = dot(wu_ref[first], later) + dot(wu_ref[second], earlier)
        taps = [z[k * cout : (k + 1) * cout] for k in range(4)]
        even = taps[1] + lane_shift(taps[3], cw, 1) + bu_ref[...]
        odd = taps[2] + lane_shift(taps[0], cw, -1) + bu_ref[...]
        parity.append((even.astype(jnp.bfloat16), odd.astype(jnp.bfloat16)))

    col = lax.broadcasted_iota(jnp.int32, (cw, fw), 0)
    pos = lax.broadcasted_iota(jnp.int32, (cw, fw), 1)
    put_even = (pos == 2 * col).astype(jnp.bfloat16)
    put_odd = (pos == 2 * col + 1).astype(jnp.bfloat16)

    joined = []
    for t in range(nfine):
        even, odd = parity[t % 2]
        q = t // 2
        row = dot(even[:, q * cw : (q + 1) * cw], put_even) + dot(odd[:, q * cw : (q + 1) * cw], put_odd)
        if t == 0:
            row = jnp.where(flags[0] == 1, 0.0, row)
        if t == nfine - 1:
            row = jnp.where(flags[1] == 1, 0.0, row)
        joined.append(jnp.concatenate([sk_ref[t], row.astype(jnp.bfloat16)], axis=0))
    field = jnp.concatenate(joined, axis=1)

    total = None
    for ky in range(3):
        part = dot(w3_ref[ky], field[:, ky * fw : (ky + nout) * fw])
        total = part if total is None else total + part
    pre = total[cout : 2 * cout]
    pre = pre + lane_shift(total[:cout], fw, 1) + lane_shift(total[2 * cout :], fw, -1)
    pre = pre + b3_ref[...]
    act = pre / (1.0 + jnp.exp(-pre))
    for y in range(nout):
        act_ref[:, y, :] = act[:, y * fw : (y + 1) * fw]
    out_ref[...] = act_ref[...].astype(out_ref.dtype)


def decode(flags, xw, sk, wu, bu, w3, b3):
    nfine, cout, fw = sk.shape
    vmem = pl.BlockSpec(memory_space=pltpu.VMEM)
    return pl.pallas_call(
        decoder_kernel,
        out_shape=jax.ShapeDtypeStruct((cout, nfine - 2, fw), jnp.bfloat16),
        in_specs=[pl.BlockSpec(memory_space=pltpu.SMEM)] + [vmem] * 6,
        out_specs=vmem,
        scratch_shapes=[pltpu.VMEM((cout, nfine - 2, fw), jnp.float32)],
        compiler_params=pltpu.CompilerParams(vmem_limit_bytes=48 * 1024 * 1024),
    )(flags, xw, sk, wu, bu, w3, b3)


def shards(coarse, skip_field, up_weight, up_bias, conv_weight, conv_bias):
    peers = lax.axis_size("row")
    me = lax.axis_index("row")
    flags = jnp.stack([me == 0, me == peers - 1]).astype(jnp.int32)
    sk = skip_rows(skip_field, peers)
    xw = coarse_windows(coarse, peers)
    cout = up_weight.shape[3]
    wu = jnp.transpose(up_weight, (0, 1, 3, 2)).reshape(4, 4 * cout, -1)
    w3 = jnp.transpose(conv_weight, (0, 1, 3, 2)).reshape(3, 3 * cout, -1)
    return decode(flags, xw, sk, wu, up_bias[:, None], w3, conv_bias[:, None])


def solution(mesh):
    in_specs = (P("row", "member", None), P(None, ("member", "row"), None), P(), P(), P(), P())
    out_specs = P(None, ("member", "row"), None)
    return jax.shard_map(shards, mesh=mesh, in_specs=in_specs, out_specs=out_specs, check_vma=False)
```

```python
import jax
import jax.numpy as jnp
from jax import lax
from jax.experimental import pallas as pl
from jax.experimental.pallas import tpu as pltpu
from jax.sharding import PartitionSpec as P


def coarse_windows(coarse, peers):
    groups, rows, cols = coarse.shape
    tile = rows // peers
    padded = jnp.pad(coarse, ((0, 0), (1, tile - 1), (0, 0)))
    blocks = padded.reshape(groups, peers + 1, tile, cols)
    windows = jnp.concatenate([blocks[:, :peers], blocks[:, 1:, :2]], axis=2)
    windows = jnp.transpose(windows, (1, 2, 0, 3))
    gathered = lax.all_to_all(windows, "row", 0, 0, tiled=True)
    if groups % 8:
        gathered = jnp.transpose(gathered, (1, 0, 2, 3)).reshape(1, tile + 2, peers * groups, cols)
    return gathered


def skip_rows(skip, peers):
    up = [(i, i + 1) for i in range(peers - 1)]
    down = [(j, i) for i, j in up]
    before = lax.ppermute(skip[:, -1:], "row", up)
    after = lax.ppermute(skip[:, :1], "row", down)
    rimmed = jnp.concatenate([before, skip, after], axis=1)
    return jnp.transpose(rimmed, (1, 0, 2))


def lane_shift(v, period, step):
    lane = lax.broadcasted_iota(jnp.int32, v.shape, 1) % period
    edge = 0 if step > 0 else period - 1
    return jnp.where(lane == edge, 0.0, pltpu.roll(v, step % v.shape[1], 1))


def decoder_kernel(flags, xw_ref, sk_ref, wu_hbm, bu_ref, w3_hbm, b3_ref, out_ref, act_ref, wu_ref, w3_ref, sems):
    loads = [pltpu.make_async_copy(wu_hbm.at[k], wu_ref.at[k], sems.at[k]) for k in range(4)]
    loads.append(pltpu.make_async_copy(w3_hbm, w3_ref, sems.at[4]))
    for load in loads:
        load.start()
    peers, nwin, groups, cw = xw_ref.shape
    nfine, cout, fw = sk_ref.shape
    nout = nfine - 2
    span = (nwin - 1) * cw
    f32 = jnp.float32

    def dot(a, b):
        return jnp.dot(a, b, preferred_element_type=f32)

    def window_row(i):
        if peers == 1:
            return xw_ref[0, i]
        pieces = [xw_ref[s, i].astype(f32) for s in range(peers)]
        return jnp.concatenate(pieces, axis=0).astype(jnp.bfloat16)

    wide = jnp.concatenate([window_row(i) for i in range(nwin)], axis=1)
    later, earlier = wide[:, cw:], wide[:, :span]
    parity = []
    for first, second in ((0, 2), (1, 3)):
        loads[first].wait()
        loads[second].wait()
        z = dot(wu_ref[first], later) + dot(wu_ref[second], earlier)
        taps = [z[k * cout : (k + 1) * cout] for k in range(4)]
        even = taps[1] + lane_shift(taps[3], cw, 1) + bu_ref[...]
        odd = taps[2] + lane_shift(taps[0], cw, -1) + bu_ref[...]
        parity.append((even.astype(jnp.bfloat16), odd.astype(jnp.bfloat16)))

    col = lax.broadcasted_iota(jnp.int32, (cw, fw), 0)
    pos = lax.broadcasted_iota(jnp.int32, (cw, fw), 1)
    put_even = (pos == 2 * col).astype(jnp.bfloat16)
    put_odd = (pos == 2 * col + 1).astype(jnp.bfloat16)

    joined = []
    for t in range(nfine):
        even, odd = parity[t % 2]
        q = t // 2
        row = dot(even[:, q * cw : (q + 1) * cw], put_even) + dot(odd[:, q * cw : (q + 1) * cw], put_odd)
        if t == 0:
            row = jnp.where(flags[0] == 1, 0.0, row)
        if t == nfine - 1:
            row = jnp.where(flags[1] == 1, 0.0, row)
        joined.append(jnp.concatenate([sk_ref[t], row.astype(jnp.bfloat16)], axis=0))
    field = jnp.concatenate(joined, axis=1)
    loads[4].wait()

    total = None
    for ky in range(3):
        part = dot(w3_ref[ky], field[:, ky * fw : (ky + nout) * fw])
        total = part if total is None else total + part
    pre = total[cout : 2 * cout]
    pre = pre + lane_shift(total[:cout], fw, 1) + lane_shift(total[2 * cout :], fw, -1)
    pre = pre + b3_ref[...]
    act = pre / (1.0 + jnp.exp(-pre))
    for y in range(nout):
        act_ref[:, y, :] = act[:, y * fw : (y + 1) * fw]
    out_ref[...] = act_ref[...].astype(out_ref.dtype)


def decode(flags, xw, sk, wu, bu, w3, b3):
    nfine, cout, fw = sk.shape
    vmem = pl.BlockSpec(memory_space=pltpu.VMEM)
    hbm = pl.BlockSpec(memory_space=pltpu.HBM)
    return pl.pallas_call(
        decoder_kernel,
        out_shape=jax.ShapeDtypeStruct((cout, nfine - 2, fw), jnp.bfloat16),
        in_specs=[pl.BlockSpec(memory_space=pltpu.SMEM), vmem, vmem, hbm, vmem, hbm, vmem],
        out_specs=vmem,
        scratch_shapes=[
            pltpu.VMEM((cout, nfine - 2, fw), jnp.float32),
            pltpu.VMEM(wu.shape, wu.dtype),
            pltpu.VMEM(w3.shape, w3.dtype),
            pltpu.SemaphoreType.DMA((5,)),
        ],
        compiler_params=pltpu.CompilerParams(vmem_limit_bytes=48 * 1024 * 1024),
    )(flags, xw, sk, pltpu.with_memory_space_constraint(wu, pltpu.HBM), bu, pltpu.with_memory_space_constraint(w3, pltpu.HBM), b3)


def shards(coarse, skip_field, up_weight, up_bias, conv_weight, conv_bias):
    peers = lax.axis_size("row")
    me = lax.axis_index("row")
    flags = jnp.stack([me == 0, me == peers - 1]).astype(jnp.int32)
    sk = skip_rows(skip_field, peers)
    xw = coarse_windows(coarse, peers)
    cout = up_weight.shape[3]
    wu = jnp.transpose(up_weight, (0, 1, 3, 2)).reshape(4, 4 * cout, -1)
    w3 = jnp.transpose(conv_weight, (0, 1, 3, 2)).reshape(3, 3 * cout, -1)
    return decode(flags, xw, sk, wu, up_bias[:, None], w3, conv_bias[:, None])


def solution(mesh):
    in_specs = (P("row", "member", None), P(None, ("member", "row"), None), P(), P(), P(), P())
    out_specs = P(None, ("member", "row"), None)
    return jax.shard_map(shards, mesh=mesh, in_specs=in_specs, out_specs=out_specs, check_vma=False)
```

```python
import jax
import jax.numpy as jnp
from jax import lax
from jax.experimental import pallas as pl
from jax.experimental.pallas import tpu as pltpu
from jax.sharding import PartitionSpec as P


def coarse_windows(coarse, peers):
    groups, rows, cols = coarse.shape
    tile = rows // peers
    padded = jnp.pad(coarse, ((0, 0), (1, tile - 1), (0, 0)))
    blocks = padded.reshape(groups, peers + 1, tile, cols)
    windows = jnp.concatenate([blocks[:, :peers], blocks[:, 1:, :2]], axis=2)
    windows = jnp.transpose(windows, (1, 2, 0, 3))
    gathered = lax.all_to_all(windows, "row", 0, 0, tiled=True)
    if groups % 8:
        gathered = jnp.transpose(gathered, (1, 0, 2, 3)).reshape(1, tile + 2, peers * groups, cols)
    return gathered


def skip_rows(skip, peers):
    up = [(i, i + 1) for i in range(peers - 1)]
    down = [(j, i) for i, j in up]
    before = lax.ppermute(skip[:, -1:], "row", up)
    after = lax.ppermute(skip[:, :1], "row", down)
    rimmed = jnp.concatenate([before, skip, after], axis=1)
    return jnp.transpose(rimmed, (1, 0, 2))


def lane_shift(v, period, step):
    lane = lax.broadcasted_iota(jnp.int32, v.shape, 1) % period
    edge = 0 if step > 0 else period - 1
    return jnp.where(lane == edge, 0.0, pltpu.roll(v, step % v.shape[1], 1))


def conv_rows(field, w_ref, nout, fw):
    total = None
    for ky in range(3):
        part = jnp.dot(w_ref[ky], field[:, ky * fw : (ky + nout) * fw], preferred_element_type=jnp.float32)
        total = part if total is None else total + part
    cout = total.shape[0] // 3
    mid = total[cout : 2 * cout]
    return mid + lane_shift(total[:cout], fw, 1) + lane_shift(total[2 * cout :], fw, -1)


def decoder_kernel(flags, xw_ref, sk_ref, wu_hbm, bu_ref, w3_hbm, b3_ref, out_ref, act_ref, wu_ref, w3_ref, sems):
    loads = {("w3", 0): pltpu.make_async_copy(w3_hbm.at[0], w3_ref.at[0], sems.at[4])}
    for k in (0, 2, 1, 3):
        loads[("wu", k)] = pltpu.make_async_copy(wu_hbm.at[k], wu_ref.at[k], sems.at[k])
    loads[("w3", 1)] = pltpu.make_async_copy(w3_hbm.at[1], w3_ref.at[1], sems.at[5])
    for load in loads.values():
        load.start()
    peers, nwin, groups, cw = xw_ref.shape
    nfine, cout, fw = sk_ref.shape
    nout = nfine - 2
    span = (nwin - 1) * cw
    f32 = jnp.float32

    def dot(a, b):
        return jnp.dot(a, b, preferred_element_type=f32)

    def window_row(i):
        if peers == 1:
            return xw_ref[0, i]
        pieces = [xw_ref[s, i].astype(f32) for s in range(peers)]
        return jnp.concatenate(pieces, axis=0).astype(jnp.bfloat16)

    skips = jnp.concatenate([sk_ref[t] for t in range(nfine)], axis=1)
    loads[("w3", 0)].wait()
    pre = conv_rows(skips, w3_ref.at[0], nout, fw) + b3_ref[...]

    wide = jnp.concatenate([window_row(i) for i in range(nwin)], axis=1)
    later, earlier = wide[:, cw:], wide[:, :span]
    parity = []
    for first, second in ((0, 2), (1, 3)):
        loads[("wu", first)].wait()
        loads[("wu", second)].wait()
        z = dot(wu_ref[first], later) + dot(wu_ref[second], earlier)
        taps = [z[k * cout : (k + 1) * cout] for k in range(4)]
        even = taps[1] + lane_shift(taps[3], cw, 1) + bu_ref[...]
        odd = taps[2] + lane_shift(taps[0], cw, -1) + bu_ref[...]
        parity.append((even.astype(jnp.bfloat16), odd.astype(jnp.bfloat16)))

    col = lax.broadcasted_iota(jnp.int32, (cw, fw), 0)
    pos = lax.broadcasted_iota(jnp.int32, (cw, fw), 1)
    put_even = (pos == 2 * col).astype(jnp.bfloat16)
    put_odd = (pos == 2 * col + 1).astype(jnp.bfloat16)

    joined = []
    for t in range(nfine):
        even, odd = parity[t % 2]
        q = t // 2
        row = dot(even[:, q * cw : (q + 1) * cw], put_even) + dot(odd[:, q * cw : (q + 1) * cw], put_odd)
        if t == 0:
            row = jnp.where(flags[0] == 1, 0.0, row)
        if t == nfine - 1:
            row = jnp.where(flags[1] == 1, 0.0, row)
        joined.append(row.astype(jnp.bfloat16))
    field = jnp.concatenate(joined, axis=1)
    loads[("w3", 1)].wait()
    pre = pre + conv_rows(field, w3_ref.at[1], nout, fw)
    act = pre / (1.0 + jnp.exp(-pre))
    for y in range(nout):
        act_ref[:, y, :] = act[:, y * fw : (y + 1) * fw]
    out_ref[...] = act_ref[...].astype(out_ref.dtype)


def decode(flags, xw, sk, wu, bu, w3, b3):
    nfine, cout, fw = sk.shape
    vmem = pl.BlockSpec(memory_space=pltpu.VMEM)
    hbm = pl.BlockSpec(memory_space=pltpu.HBM)
    return pl.pallas_call(
        decoder_kernel,
        out_shape=jax.ShapeDtypeStruct((cout, nfine - 2, fw), jnp.bfloat16),
        in_specs=[pl.BlockSpec(memory_space=pltpu.SMEM), vmem, vmem, hbm, vmem, hbm, vmem],
        out_specs=vmem,
        scratch_shapes=[
            pltpu.VMEM((cout, nfine - 2, fw), jnp.float32),
            pltpu.VMEM(wu.shape, wu.dtype),
            pltpu.VMEM(w3.shape, w3.dtype),
            pltpu.SemaphoreType.DMA((6,)),
        ],
        compiler_params=pltpu.CompilerParams(vmem_limit_bytes=48 * 1024 * 1024),
    )(flags, xw, sk, pltpu.with_memory_space_constraint(wu, pltpu.HBM), bu, pltpu.with_memory_space_constraint(w3, pltpu.HBM), b3)


def shards(coarse, skip_field, up_weight, up_bias, conv_weight, conv_bias):
    peers = lax.axis_size("row")
    me = lax.axis_index("row")
    flags = jnp.stack([me == 0, me == peers - 1]).astype(jnp.int32)
    sk = skip_rows(skip_field, peers)
    xw = coarse_windows(coarse, peers)
    cout = up_weight.shape[3]
    wu = jnp.transpose(up_weight, (0, 1, 3, 2)).reshape(4, 4 * cout, -1)
    halves = conv_weight.reshape(3, 3, 2, -1, cout)
    w3 = jnp.transpose(halves, (2, 0, 1, 4, 3)).reshape(2, 3, 3 * cout, -1)
    return decode(flags, xw, sk, wu, up_bias[:, None], w3, conv_bias[:, None])


def solution(mesh):
    in_specs = (P("row", "member", None), P(None, ("member", "row"), None), P(), P(), P(), P())
    out_specs = P(None, ("member", "row"), None)
    return jax.shard_map(shards, mesh=mesh, in_specs=in_specs, out_specs=out_specs, check_vma=False)
```

```python
import jax
import jax.numpy as jnp
from jax import lax
from jax.experimental import pallas as pl
from jax.experimental.pallas import tpu as pltpu
from jax.sharding import PartitionSpec as P


def coarse_windows(coarse, peers):
    groups, rows, cols = coarse.shape
    tile = rows // peers
    padded = jnp.pad(coarse, ((0, 0), (1, tile - 1), (0, 0)))
    blocks = padded.reshape(groups, peers + 1, tile, cols)
    windows = jnp.concatenate([blocks[:, :peers], blocks[:, 1:, :2]], axis=2)
    windows = jnp.transpose(windows, (1, 2, 0, 3))
    gathered = lax.all_to_all(windows, "row", 0, 0, tiled=True)
    if groups % 8:
        gathered = jnp.transpose(gathered, (1, 0, 2, 3)).reshape(1, tile + 2, peers * groups, cols)
    return gathered


def skip_rows(skip, peers):
    up = [(i, i + 1) for i in range(peers - 1)]
    down = [(j, i) for i, j in up]
    before = lax.ppermute(skip[:, -1:], "row", up)
    after = lax.ppermute(skip[:, :1], "row", down)
    rimmed = jnp.concatenate([before, skip, after], axis=1)
    return jnp.transpose(rimmed, (1, 0, 2))


def lane_shift(v, period, step):
    lane = lax.broadcasted_iota(jnp.int32, v.shape, 1) % period
    edge = 0 if step > 0 else period - 1
    return jnp.where(lane == edge, 0.0, pltpu.roll(v, step % v.shape[1], 1))


def decoder_kernel(flags, xw_ref, sk_ref, wu_hbm, bu_ref, w3_hbm, b3_ref, out_ref, act_ref, wu_ref, w3_ref, sems):
    loads = [pltpu.make_async_copy(wu_hbm.at[k], wu_ref.at[k], sems.at[k]) for k in range(2)]
    loads.append(pltpu.make_async_copy(w3_hbm, w3_ref, sems.at[2]))
    for load in loads:
        load.start()
    peers, nwin, groups, cw = xw_ref.shape
    nfine, cout, fw = sk_ref.shape
    nout = nfine - 2
    span = (nwin - 1) * cw
    f32 = jnp.float32

    def dot(a, b):
        return jnp.dot(a, b, preferred_element_type=f32)

    def window_row(i):
        if peers == 1:
            return xw_ref[0, i]
        pieces = [xw_ref[s, i].astype(f32) for s in range(peers)]
        return jnp.concatenate(pieces, axis=0).astype(jnp.bfloat16)

    wide = jnp.concatenate([window_row(i) for i in range(nwin)], axis=1)
    stacked = jnp.concatenate([wide[:, cw:], wide[:, :span]], axis=0)
    parity = []
    for p in range(2):
        loads[p].wait()
        z = dot(wu_ref[p], stacked)
        taps = [z[k * cout : (k + 1) * cout] for k in range(4)]
        even = taps[1] + lane_shift(taps[3], cw, 1) + bu_ref[...]
        odd = taps[2] + lane_shift(taps[0], cw, -1) + bu_ref[...]
        parity.append((even.astype(jnp.bfloat16), odd.astype(jnp.bfloat16)))

    col = lax.broadcasted_iota(jnp.int32, (cw, fw), 0)
    pos = lax.broadcasted_iota(jnp.int32, (cw, fw), 1)
    put_even = (pos == 2 * col).astype(jnp.bfloat16)
    put_odd = (pos == 2 * col + 1).astype(jnp.bfloat16)

    joined = []
    for t in range(nfine):
        even, odd = parity[t % 2]
        q = t // 2
        row = dot(even[:, q * cw : (q + 1) * cw], put_even) + dot(odd[:, q * cw : (q + 1) * cw], put_odd)
        if t == 0:
            row = jnp.where(flags[0] == 1, 0.0, row)
        if t == nfine - 1:
            row = jnp.where(flags[1] == 1, 0.0, row)
        joined.append(jnp.concatenate([sk_ref[t], row.astype(jnp.bfloat16)], axis=0))
    field = jnp.concatenate(joined, axis=1)
    loads[2].wait()

    rows = jnp.concatenate([field[:, ky * fw : (ky + nout) * fw] for ky in range(3)], axis=0)
    total = dot(w3_ref[...], rows)
    pre = total[cout : 2 * cout]
    pre = pre + lane_shift(total[:cout], fw, 1) + lane_shift(total[2 * cout :], fw, -1)
    pre = pre + b3_ref[...]
    act = pre / (1.0 + jnp.exp(-pre))
    for y in range(nout):
        act_ref[:, y, :] = act[:, y * fw : (y + 1) * fw]
    out_ref[...] = act_ref[...].astype(out_ref.dtype)


def decode(flags, xw, sk, wu, bu, w3, b3):
    nfine, cout, fw = sk.shape
    vmem = pl.BlockSpec(memory_space=pltpu.VMEM)
    hbm = pl.BlockSpec(memory_space=pltpu.HBM)
    return pl.pallas_call(
        decoder_kernel,
        out_shape=jax.ShapeDtypeStruct((cout, nfine - 2, fw), jnp.bfloat16),
        in_specs=[pl.BlockSpec(memory_space=pltpu.SMEM), vmem, vmem, hbm, vmem, hbm, vmem],
        out_specs=vmem,
        scratch_shapes=[
            pltpu.VMEM((cout, nfine - 2, fw), jnp.float32),
            pltpu.VMEM(wu.shape, wu.dtype),
            pltpu.VMEM(w3.shape, w3.dtype),
            pltpu.SemaphoreType.DMA((3,)),
        ],
        compiler_params=pltpu.CompilerParams(vmem_limit_bytes=48 * 1024 * 1024),
    )(flags, xw, sk, pltpu.with_memory_space_constraint(wu, pltpu.HBM), bu, pltpu.with_memory_space_constraint(w3, pltpu.HBM), b3)


def shards(coarse, skip_field, up_weight, up_bias, conv_weight, conv_bias):
    peers = lax.axis_size("row")
    me = lax.axis_index("row")
    flags = jnp.stack([me == 0, me == peers - 1]).astype(jnp.int32)
    sk = skip_rows(skip_field, peers)
    xw = coarse_windows(coarse, peers)
    cout = up_weight.shape[3]
    wu = jnp.transpose(up_weight.reshape(2, 2, 4, -1, cout), (1, 2, 4, 0, 3)).reshape(2, 4 * cout, -1)
    w3 = jnp.transpose(conv_weight, (1, 3, 0, 2)).reshape(3 * cout, -1)
    return decode(flags, xw, sk, wu, up_bias[:, None], w3, conv_bias[:, None])


def solution(mesh):
    in_specs = (P("row", "member", None), P(None, ("member", "row"), None), P(), P(), P(), P())
    out_specs = P(None, ("member", "row"), None)
    return jax.shard_map(shards, mesh=mesh, in_specs=in_specs, out_specs=out_specs, check_vma=False)
```

```python
import jax
import jax.numpy as jnp
from jax import lax
from jax.experimental import pallas as pl
from jax.experimental.pallas import tpu as pltpu
from jax.sharding import PartitionSpec as P


def coarse_windows(coarse, peers):
    groups, rows, cols = coarse.shape
    tile = rows // peers
    padded = jnp.pad(coarse, ((0, 0), (1, tile - 1), (0, 0)))
    blocks = padded.reshape(groups, peers + 1, tile, cols)
    windows = jnp.concatenate([blocks[:, :peers], blocks[:, 1:, :2]], axis=2)
    windows = jnp.transpose(windows, (1, 2, 0, 3))
    gathered = lax.all_to_all(windows, "row", 0, 0, tiled=True)
    if groups % 8:
        gathered = jnp.transpose(gathered, (1, 0, 2, 3)).reshape(1, tile + 2, peers * groups, cols)
    return gathered


def skip_rows(skip, peers):
    up = [(i, i + 1) for i in range(peers - 1)]
    down = [(j, i) for i, j in up]
    before = lax.ppermute(skip[:, -1:], "row", up)
    after = lax.ppermute(skip[:, :1], "row", down)
    rimmed = jnp.concatenate([before, skip, after], axis=1)
    return jnp.transpose(rimmed, (1, 0, 2))


def lane_shift(v, period, step):
    lane = lax.broadcasted_iota(jnp.int32, v.shape, 1) % period
    edge = 0 if step > 0 else period - 1
    return jnp.where(lane == edge, 0.0, pltpu.roll(v, step % v.shape[1], 1))


def decoder_kernel(flags, xw_ref, sk_ref, wu_hbm, bu_ref, w3_hbm, b3_ref, out_ref, act_ref, wu_ref, w3_ref, sems):
    cin = wu_hbm.shape[2]

    def load(src, dst, k):
        copy = pltpu.make_async_copy(src, dst, sems.at[k])
        copy.start()
        return copy

    up_loads = [[load(wu_hbm.at[p + 2 * h], wu_ref.at[p, :, pl.ds(h * cin, cin)], 2 * p + h) for h in range(2)] for p in range(2)]
    conv_loads = [load(w3_hbm.at[ky], w3_ref.at[:, pl.ds(ky * cin, cin)], 4 + ky) for ky in range(3)]
    peers, nwin, groups, cw = xw_ref.shape
    nfine, cout, fw = sk_ref.shape
    nout = nfine - 2
    span = (nwin - 1) * cw
    f32 = jnp.float32

    def dot(a, b):
        return jnp.dot(a, b, preferred_element_type=f32)

    def window_row(i):
        if peers == 1:
            return xw_ref[0, i]
        pieces = [xw_ref[s, i].astype(f32) for s in range(peers)]
        return jnp.concatenate(pieces, axis=0).astype(jnp.bfloat16)

    wide = jnp.concatenate([window_row(i) for i in range(nwin)], axis=1)
    stacked = jnp.concatenate([wide[:, cw:], wide[:, :span]], axis=0)
    parity = []
    for p in range(2):
        for copy in up_loads[p]:
            copy.wait()
        z = dot(wu_ref[p], stacked)
        taps = [z[k * cout : (k + 1) * cout] for k in range(4)]
        even = taps[1] + lane_shift(taps[3], cw, 1) + bu_ref[...]
        odd = taps[2] + lane_shift(taps[0], cw, -1) + bu_ref[...]
        parity.append((even.astype(jnp.bfloat16), odd.astype(jnp.bfloat16)))

    col = lax.broadcasted_iota(jnp.int32, (cw, fw), 0)
    pos = lax.broadcasted_iota(jnp.int32, (cw, fw), 1)
    put_even = (pos == 2 * col).astype(jnp.bfloat16)
    put_odd = (pos == 2 * col + 1).astype(jnp.bfloat16)

    joined = []
    for t in range(nfine):
        even, odd = parity[t % 2]
        q = t // 2
        row = dot(even[:, q * cw : (q + 1) * cw], put_even) + dot(odd[:, q * cw : (q + 1) * cw], put_odd)
        if t == 0:
            row = jnp.where(flags[0] == 1, 0.0, row)
        if t == nfine - 1:
            row = jnp.where(flags[1] == 1, 0.0, row)
        joined.append(jnp.concatenate([sk_ref[t], row.astype(jnp.bfloat16)], axis=0))
    field = jnp.concatenate(joined, axis=1)
    for copy in conv_loads:
        copy.wait()

    rows = jnp.concatenate([field[:, ky * fw : (ky + nout) * fw] for ky in range(3)], axis=0)
    total = dot(w3_ref[...], rows)
    pre = total[cout : 2 * cout]
    pre = pre + lane_shift(total[:cout], fw, 1) + lane_shift(total[2 * cout :], fw, -1)
    pre = pre + b3_ref[...]
    act = pre / (1.0 + jnp.exp(-pre))
    for y in range(nout):
        act_ref[:, y, :] = act[:, y * fw : (y + 1) * fw]
    out_ref[...] = act_ref[...].astype(out_ref.dtype)


def decode(flags, xw, sk, wu, bu, w3, b3):
    nfine, cout, fw = sk.shape
    vmem = pl.BlockSpec(memory_space=pltpu.VMEM)
    hbm = pl.BlockSpec(memory_space=pltpu.HBM)
    return pl.pallas_call(
        decoder_kernel,
        out_shape=jax.ShapeDtypeStruct((cout, nfine - 2, fw), jnp.bfloat16),
        in_specs=[pl.BlockSpec(memory_space=pltpu.SMEM), vmem, vmem, hbm, vmem, hbm, vmem],
        out_specs=vmem,
        scratch_shapes=[
            pltpu.VMEM((cout, nfine - 2, fw), jnp.float32),
            pltpu.VMEM((2, wu.shape[1], 2 * wu.shape[2]), wu.dtype),
            pltpu.VMEM((w3.shape[1], 3 * w3.shape[2]), w3.dtype),
            pltpu.SemaphoreType.DMA((7,)),
        ],
        compiler_params=pltpu.CompilerParams(vmem_limit_bytes=48 * 1024 * 1024),
    )(flags, xw, sk, pltpu.with_memory_space_constraint(wu, pltpu.HBM), bu, pltpu.with_memory_space_constraint(w3, pltpu.HBM), b3)


def shards(coarse, skip_field, up_weight, up_bias, conv_weight, conv_bias):
    peers = lax.axis_size("row")
    me = lax.axis_index("row")
    flags = jnp.stack([me == 0, me == peers - 1]).astype(jnp.int32)
    sk = skip_rows(skip_field, peers)
    xw = coarse_windows(coarse, peers)
    cout = up_weight.shape[3]
    wu = jnp.transpose(up_weight, (0, 1, 3, 2)).reshape(4, 4 * cout, -1)
    w3 = jnp.transpose(conv_weight, (0, 1, 3, 2)).reshape(3, 3 * cout, -1)
    return decode(flags, xw, sk, wu, up_bias[:, None], w3, conv_bias[:, None])


def solution(mesh):
    in_specs = (P("row", "member", None), P(None, ("member", "row"), None), P(), P(), P(), P())
    out_specs = P(None, ("member", "row"), None)
    return jax.shard_map(shards, mesh=mesh, in_specs=in_specs, out_specs=out_specs, check_vma=False)
```

```python
import jax
import jax.numpy as jnp
from jax import lax
from jax.experimental import pallas as pl
from jax.experimental.pallas import tpu as pltpu
from jax.sharding import PartitionSpec as P


def coarse_windows(coarse, peers):
    groups, rows, cols = coarse.shape
    tile = rows // peers
    padded = jnp.pad(coarse, ((0, 0), (1, tile - 1), (0, 0)))
    blocks = padded.reshape(groups, peers + 1, tile, cols)
    windows = jnp.concatenate([blocks[:, :peers], blocks[:, 1:, :2]], axis=2)
    windows = jnp.transpose(windows, (1, 2, 0, 3))
    gathered = lax.all_to_all(windows, "row", 0, 0, tiled=True)
    if groups % 8:
        gathered = jnp.transpose(gathered, (1, 0, 2, 3)).reshape(1, tile + 2, peers * groups, cols)
    return gathered


def skip_rows(skip, peers):
    up = [(i, i + 1) for i in range(peers - 1)]
    down = [(j, i) for i, j in up]
    before = lax.ppermute(skip[:, -1:], "row", up)
    after = lax.ppermute(skip[:, :1], "row", down)
    rimmed = jnp.concatenate([before, skip, after], axis=1)
    return jnp.transpose(rimmed, (1, 0, 2))


def lane_shift(v, period, step):
    lane = lax.broadcasted_iota(jnp.int32, v.shape, 1) % period
    edge = 0 if step > 0 else period - 1
    return jnp.where(lane == edge, 0.0, pltpu.roll(v, step % v.shape[1], 1))


def conv_rows(field, w, nout, fw):
    rows = jnp.concatenate([field[:, ky * fw : (ky + nout) * fw] for ky in range(3)], axis=0)
    total = jnp.dot(w, rows, preferred_element_type=jnp.float32)
    cout = total.shape[0] // 3
    mid = total[cout : 2 * cout]
    return mid + lane_shift(total[:cout], fw, 1) + lane_shift(total[2 * cout :], fw, -1)


def skip_kernel(sk_ref, w_ref, b_ref, out_ref):
    nfine, _, fw = sk_ref.shape
    field = jnp.concatenate([sk_ref[t] for t in range(nfine)], axis=1)
    out_ref[...] = conv_rows(field, w_ref[...], nfine - 2, fw) + b_ref[...]


def decoder_kernel(flags, xw_ref, part_hbm, wu_hbm, bu_ref, w3_hbm, out_ref, act_ref, part_ref, wu_ref, w3_ref, sems):
    cin = wu_hbm.shape[2]

    def load(src, dst, k):
        copy = pltpu.make_async_copy(src, dst, sems.at[k])
        copy.start()
        return copy

    up_loads = [[load(wu_hbm.at[p + 2 * h], wu_ref.at[p, :, pl.ds(h * cin, cin)], 2 * p + h) for h in range(2)] for p in range(2)]
    conv_load = load(w3_hbm, w3_ref, 4)
    part_load = load(part_hbm, part_ref, 5)
    peers, nwin, groups, cw = xw_ref.shape
    cout, nout, fw = out_ref.shape
    nfine = nout + 2
    span = (nwin - 1) * cw
    f32 = jnp.float32

    def dot(a, b):
        return jnp.dot(a, b, preferred_element_type=f32)

    def window_row(i):
        if peers == 1:
            return xw_ref[0, i]
        pieces = [xw_ref[s, i].astype(f32) for s in range(peers)]
        return jnp.concatenate(pieces, axis=0).astype(jnp.bfloat16)

    wide = jnp.concatenate([window_row(i) for i in range(nwin)], axis=1)
    stacked = jnp.concatenate([wide[:, cw:], wide[:, :span]], axis=0)
    parity = []
    for p in range(2):
        for copy in up_loads[p]:
            copy.wait()
        z = dot(wu_ref[p], stacked)
        taps = [z[k * cout : (k + 1) * cout] for k in range(4)]
        even = taps[1] + lane_shift(taps[3], cw, 1) + bu_ref[...]
        odd = taps[2] + lane_shift(taps[0], cw, -1) + bu_ref[...]
        parity.append((even.astype(jnp.bfloat16), odd.astype(jnp.bfloat16)))

    col = lax.broadcasted_iota(jnp.int32, (cw, fw), 0)
    pos = lax.broadcasted_iota(jnp.int32, (cw, fw), 1)
    put_even = (pos == 2 * col).astype(jnp.bfloat16)
    put_odd = (pos == 2 * col + 1).astype(jnp.bfloat16)

    joined = []
    for t in range(nfine):
        even, odd = parity[t % 2]
        q = t // 2
        row = dot(even[:, q * cw : (q + 1) * cw], put_even) + dot(odd[:, q * cw : (q + 1) * cw], put_odd)
        if t == 0:
            row = jnp.where(flags[0] == 1, 0.0, row)
        if t == nfine - 1:
            row = jnp.where(flags[1] == 1, 0.0, row)
        joined.append(row.astype(jnp.bfloat16))
    field = jnp.concatenate(joined, axis=1)
    conv_load.wait()
    pre = conv_rows(field, w3_ref[...], nout, fw)
    part_load.wait()
    pre = pre + part_ref[...]
    act = pre / (1.0 + jnp.exp(-pre))
    for y in range(nout):
        act_ref[:, y, :] = act[:, y * fw : (y + 1) * fw]
    out_ref[...] = act_ref[...].astype(out_ref.dtype)


def skip_conv(sk, w3s, b3):
    nfine, cout, fw = sk.shape
    nout = nfine - 2
    vmem = pl.BlockSpec(memory_space=pltpu.VMEM)
    flops = 2 * w3s.shape[0] * w3s.shape[1] * nout * fw
    moved = sk.size * 2 + w3s.size * 2 + cout * nout * fw * 4
    return pl.pallas_call(
        skip_kernel,
        out_shape=jax.ShapeDtypeStruct((cout, nout * fw), jnp.float32),
        in_specs=[vmem] * 3,
        out_specs=vmem,
        compiler_params=pltpu.CompilerParams(vmem_limit_bytes=48 * 1024 * 1024),
        cost_estimate=pl.CostEstimate(flops=flops, transcendentals=0, bytes_accessed=moved),
    )(sk, w3s, b3)


def decode(flags, xw, part, wu, bu, w3u, nout, fw):
    cout = bu.shape[0]
    vmem = pl.BlockSpec(memory_space=pltpu.VMEM)
    hbm = pl.BlockSpec(memory_space=pltpu.HBM)
    in_hbm = lambda x: pltpu.with_memory_space_constraint(x, pltpu.HBM)
    return pl.pallas_call(
        decoder_kernel,
        out_shape=jax.ShapeDtypeStruct((cout, nout, fw), jnp.bfloat16),
        in_specs=[pl.BlockSpec(memory_space=pltpu.SMEM), vmem, hbm, hbm, vmem, hbm],
        out_specs=vmem,
        scratch_shapes=[
            pltpu.VMEM((cout, nout, fw), jnp.float32),
            pltpu.VMEM(part.shape, part.dtype),
            pltpu.VMEM((2, wu.shape[1], 2 * wu.shape[2]), wu.dtype),
            pltpu.VMEM(w3u.shape, w3u.dtype),
            pltpu.SemaphoreType.DMA((6,)),
        ],
        compiler_params=pltpu.CompilerParams(vmem_limit_bytes=48 * 1024 * 1024),
    )(flags, xw, in_hbm(part), in_hbm(wu), bu, in_hbm(w3u))


def shards(coarse, skip_field, up_weight, up_bias, conv_weight, conv_bias):
    peers = lax.axis_size("row")
    me = lax.axis_index("row")
    flags = jnp.stack([me == 0, me == peers - 1]).astype(jnp.int32)
    sk = skip_rows(skip_field, peers)
    xw = coarse_windows(coarse, peers)
    cout = up_weight.shape[3]
    wu = jnp.transpose(up_weight, (0, 1, 3, 2)).reshape(4, 4 * cout, -1)
    skips = skip_field.shape[0]
    halves = conv_weight.reshape(3, 3, 2, skips, cout)
    w3 = jnp.transpose(halves, (2, 1, 4, 0, 3)).reshape(2, 3 * cout, 3 * skips)
    part = skip_conv(sk, w3[0], conv_bias[:, None])
    nout, fw = skip_field.shape[1], skip_field.shape[2]
    return decode(flags, xw, part, wu, up_bias[:, None], w3[1], nout, fw)


def solution(mesh):
    in_specs = (P("row", "member", None), P(None, ("member", "row"), None), P(), P(), P(), P())
    out_specs = P(None, ("member", "row"), None)
    return jax.shard_map(shards, mesh=mesh, in_specs=in_specs, out_specs=out_specs, check_vma=False)
```

```python
import jax
import jax.numpy as jnp
from jax import lax
from jax.experimental import pallas as pl
from jax.experimental.pallas import tpu as pltpu
from jax.sharding import PartitionSpec as P


def coarse_windows(coarse, peers):
    groups, rows, cols = coarse.shape
    tile = rows // peers
    padded = jnp.pad(coarse, ((0, 0), (1, tile - 1), (0, 0)))
    blocks = padded.reshape(groups, peers + 1, tile, cols)
    windows = jnp.concatenate([blocks[:, :peers], blocks[:, 1:, :2]], axis=2)
    windows = jnp.transpose(windows, (1, 2, 0, 3))
    gathered = lax.all_to_all(windows, "row", 0, 0, tiled=True)
    if groups % 8:
        gathered = jnp.transpose(gathered, (1, 0, 2, 3)).reshape(1, tile + 2, peers * groups, cols)
    return gathered


def skip_rows(skip, peers):
    up = [(i, i + 1) for i in range(peers - 1)]
    down = [(j, i) for i, j in up]
    before = lax.ppermute(skip[:, -1:], "row", up)
    after = lax.ppermute(skip[:, :1], "row", down)
    rimmed = jnp.concatenate([before, skip, after], axis=1)
    return jnp.transpose(rimmed, (1, 0, 2))


def lane_shift(v, period, step):
    lane = lax.broadcasted_iota(jnp.int32, v.shape, 1) % period
    edge = 0 if step > 0 else period - 1
    return jnp.where(lane == edge, 0.0, pltpu.roll(v, step % v.shape[1], 1))


def decoder_kernel(flags, xw_ref, sk_ref, wu_hbm, bu_ref, w3_hbm, b3_ref, out_ref, act_ref, wu_ref, w3_ref, sems):
    cin = wu_hbm.shape[2]

    def load(src, dst, k):
        copy = pltpu.make_async_copy(src, dst, sems.at[k])
        copy.start()
        return copy

    up_loads = [[load(wu_hbm.at[p + 2 * h], wu_ref.at[p, :, pl.ds(h * cin, cin)], 2 * p + h) for h in range(2)] for p in range(2)]
    conv_loads = [load(w3_hbm.at[ky], w3_ref.at[:, pl.ds(ky * cin, cin)], 4 + ky) for ky in range(3)]
    peers, nwin, groups, cw = xw_ref.shape
    nfine, cout, fw = sk_ref.shape
    nout = nfine - 2
    span = (nwin - 1) * cw
    f32 = jnp.float32

    def dot(a, b):
        return jnp.dot(a, b, preferred_element_type=f32)

    def window_row(i):
        if peers == 1:
            return xw_ref[0, i]
        pieces = [xw_ref[s, i].astype(f32) for s in range(peers)]
        return jnp.concatenate(pieces, axis=0).astype(jnp.bfloat16)

    wide = jnp.concatenate([window_row(i) for i in range(nwin)], axis=1)
    stacked = jnp.concatenate([wide[:, cw:], wide[:, :span]], axis=0)
    parity = []
    for p in range(2):
        for copy in up_loads[p]:
            copy.wait()
        z = dot(wu_ref[p], stacked)
        taps = [z[k * cout : (k + 1) * cout] for k in range(4)]
        even = taps[1] + lane_shift(taps[3], cw, 1) + bu_ref[...]
        odd = taps[2] + lane_shift(taps[0], cw, -1) + bu_ref[...]
        parity.append((even.astype(jnp.bfloat16), odd.astype(jnp.bfloat16)))

    col = lax.broadcasted_iota(jnp.int32, (cw, fw), 0)
    pos = lax.broadcasted_iota(jnp.int32, (cw, fw), 1)
    put_even = (pos == 2 * col).astype(jnp.bfloat16)
    put_odd = (pos == 2 * col + 1).astype(jnp.bfloat16)
    put = jnp.concatenate([put_even, put_odd], axis=0)

    joined = []
    for t in range(nfine):
        even, odd = parity[t % 2]
        q = t // 2
        pair = jnp.concatenate([even[:, q * cw : (q + 1) * cw], odd[:, q * cw : (q + 1) * cw]], axis=1)
        row = dot(pair, put)
        if t == 0:
            row = jnp.where(flags[0] == 1, 0.0, row)
        if t == nfine - 1:
            row = jnp.where(flags[1] == 1, 0.0, row)
        joined.append(jnp.concatenate([sk_ref[t], row.astype(jnp.bfloat16)], axis=0))
    field = jnp.concatenate(joined, axis=1)
    for copy in conv_loads:
        copy.wait()

    rows = jnp.concatenate([field[:, ky * fw : (ky + nout) * fw] for ky in range(3)], axis=0)
    total = dot(w3_ref[...], rows)
    pre = total[cout : 2 * cout]
    pre = pre + lane_shift(total[:cout], fw, 1) + lane_shift(total[2 * cout :], fw, -1)
    pre = pre + b3_ref[...]
    act = pre / (1.0 + jnp.exp(-pre))
    for y in range(nout):
        act_ref[:, y, :] = act[:, y * fw : (y + 1) * fw]
    out_ref[...] = act_ref[...].astype(out_ref.dtype)


def decode(flags, xw, sk, wu, bu, w3, b3):
    nfine, cout, fw = sk.shape
    vmem = pl.BlockSpec(memory_space=pltpu.VMEM)
    hbm = pl.BlockSpec(memory_space=pltpu.HBM)
    return pl.pallas_call(
        decoder_kernel,
        out_shape=jax.ShapeDtypeStruct((cout, nfine - 2, fw), jnp.bfloat16),
        in_specs=[pl.BlockSpec(memory_space=pltpu.SMEM), vmem, vmem, hbm, vmem, hbm, vmem],
        out_specs=vmem,
        scratch_shapes=[
            pltpu.VMEM((cout, nfine - 2, fw), jnp.float32),
            pltpu.VMEM((2, wu.shape[1], 2 * wu.shape[2]), wu.dtype),
            pltpu.VMEM((w3.shape[1], 3 * w3.shape[2]), w3.dtype),
            pltpu.SemaphoreType.DMA((7,)),
        ],
        compiler_params=pltpu.CompilerParams(vmem_limit_bytes=48 * 1024 * 1024),
    )(flags, xw, sk, pltpu.with_memory_space_constraint(wu, pltpu.HBM), bu, pltpu.with_memory_space_constraint(w3, pltpu.HBM), b3)


def shards(coarse, skip_field, up_weight, up_bias, conv_weight, conv_bias):
    peers = lax.axis_size("row")
    me = lax.axis_index("row")
    flags = jnp.stack([me == 0, me == peers - 1]).astype(jnp.int32)
    sk = skip_rows(skip_field, peers)
    xw = coarse_windows(coarse, peers)
    cout = up_weight.shape[3]
    wu = jnp.transpose(up_weight, (0, 1, 3, 2)).reshape(4, 4 * cout, -1)
    w3 = jnp.transpose(conv_weight, (0, 1, 3, 2)).reshape(3, 3 * cout, -1)
    return decode(flags, xw, sk, wu, up_bias[:, None], w3, conv_bias[:, None])


def solution(mesh):
    in_specs = (P("row", "member", None), P(None, ("member", "row"), None), P(), P(), P(), P())
    out_specs = P(None, ("member", "row"), None)
    return jax.shard_map(shards, mesh=mesh, in_specs=in_specs, out_specs=out_specs, check_vma=False)
```

```python
import jax
import jax.numpy as jnp
from jax import lax
from jax.experimental import pallas as pl
from jax.experimental.pallas import tpu as pltpu
from jax.sharding import PartitionSpec as P


def coarse_windows(coarse, peers):
    groups, rows, cols = coarse.shape
    tile = rows // peers
    padded = jnp.pad(coarse, ((0, 0), (1, tile - 1), (0, 0)))
    blocks = padded.reshape(groups, peers + 1, tile, cols)
    windows = jnp.concatenate([blocks[:, :peers], blocks[:, 1:, :2]], axis=2)
    windows = jnp.transpose(windows, (1, 2, 0, 3))
    gathered = lax.all_to_all(windows, "row", 0, 0, tiled=True)
    if groups % 8:
        gathered = jnp.transpose(gathered, (1, 0, 2, 3)).reshape(1, tile + 2, peers * groups, cols)
    return gathered


def skip_rows(skip, peers):
    up = [(i, i + 1) for i in range(peers - 1)]
    down = [(j, i) for i, j in up]
    before = lax.ppermute(skip[:, -1:], "row", up)
    after = lax.ppermute(skip[:, :1], "row", down)
    rimmed = jnp.concatenate([before, skip, after], axis=1)
    return jnp.transpose(rimmed, (1, 0, 2))


def lane_shift(v, period, step):
    lane = lax.broadcasted_iota(jnp.int32, v.shape, 1)
    lane = lane & (period - 1) if period & (period - 1) == 0 else lane % period
    edge = 0 if step > 0 else period - 1
    return jnp.where(lane == edge, 0.0, pltpu.roll(v, step % v.shape[1], 1))


def decoder_kernel(flags, xw_ref, sk_ref, wu_hbm, bu_ref, w3_hbm, b3_ref, out_ref, act_ref, wu_ref, w3_ref, sems):
    cin = wu_hbm.shape[2]

    def load(src, dst, k):
        copy = pltpu.make_async_copy(src, dst, sems.at[k])
        copy.start()
        return copy

    up_loads = [[load(wu_hbm.at[p + 2 * h], wu_ref.at[p, :, pl.ds(h * cin, cin)], 2 * p + h) for h in range(2)] for p in range(2)]
    conv_loads = [load(w3_hbm.at[ky], w3_ref.at[:, pl.ds(ky * cin, cin)], 4 + ky) for ky in range(3)]
    peers, nwin, groups, cw = xw_ref.shape
    nfine, cout, fw = sk_ref.shape
    nout = nfine - 2
    span = (nwin - 1) * cw
    f32 = jnp.float32

    def dot(a, b):
        return jnp.dot(a, b, preferred_element_type=f32)

    def window_row(i):
        if peers == 1:
            return xw_ref[0, i]
        pieces = [xw_ref[s, i].astype(f32) for s in range(peers)]
        return jnp.concatenate(pieces, axis=0).astype(jnp.bfloat16)

    wide = jnp.concatenate([window_row(i) for i in range(nwin)], axis=1)
    stacked = jnp.concatenate([wide[:, cw:], wide[:, :span]], axis=0)
    parity = []
    for p in range(2):
        for copy in up_loads[p]:
            copy.wait()
        z = dot(wu_ref[p], stacked)
        taps = [z[k * cout : (k + 1) * cout] for k in range(4)]
        even = taps[1] + lane_shift(taps[3], cw, 1) + bu_ref[...]
        odd = taps[2] + lane_shift(taps[0], cw, -1) + bu_ref[...]
        parity.append((even.astype(jnp.bfloat16), odd.astype(jnp.bfloat16)))

    col = lax.broadcasted_iota(jnp.int32, (cw, fw), 0)
    pos = lax.broadcasted_iota(jnp.int32, (cw, fw), 1)
    put_even = (pos == 2 * col).astype(jnp.bfloat16)
    put_odd = (pos == 2 * col + 1).astype(jnp.bfloat16)
    put = jnp.concatenate([put_even, put_odd], axis=0)

    joined = []
    for t in range(nfine):
        even, odd = parity[t % 2]
        q = t // 2
        pair = jnp.concatenate([even[:, q * cw : (q + 1) * cw], odd[:, q * cw : (q + 1) * cw]], axis=1)
        row = dot(pair, put)
        if t == 0:
            row = jnp.where(flags[0] == 1, 0.0, row)
        if t == nfine - 1:
            row = jnp.where(flags[1] == 1, 0.0, row)
        joined.append(jnp.concatenate([sk_ref[t], row.astype(jnp.bfloat16)], axis=0))
    field = jnp.concatenate(joined, axis=1)
    for copy in conv_loads:
        copy.wait()

    rows = jnp.concatenate([field[:, ky * fw : (ky + nout) * fw] for ky in range(3)], axis=0)
    total = dot(w3_ref[...], rows)
    pre = total[cout : 2 * cout]
    pre = pre + lane_shift(total[:cout], fw, 1) + lane_shift(total[2 * cout :], fw, -1)
    pre = pre + b3_ref[...]
    act = pre / (1.0 + jnp.exp(-pre))
    for y in range(nout):
        act_ref[:, y, :] = act[:, y * fw : (y + 1) * fw]
    out_ref[...] = act_ref[...].astype(out_ref.dtype)


def decode(flags, xw, sk, wu, bu, w3, b3):
    nfine, cout, fw = sk.shape
    vmem = pl.BlockSpec(memory_space=pltpu.VMEM)
    hbm = pl.BlockSpec(memory_space=pltpu.HBM)
    return pl.pallas_call(
        decoder_kernel,
        out_shape=jax.ShapeDtypeStruct((cout, nfine - 2, fw), jnp.bfloat16),
        in_specs=[pl.BlockSpec(memory_space=pltpu.SMEM), vmem, vmem, hbm, vmem, hbm, vmem],
        out_specs=vmem,
        scratch_shapes=[
            pltpu.VMEM((cout, nfine - 2, fw), jnp.float32),
            pltpu.VMEM((2, wu.shape[1], 2 * wu.shape[2]), wu.dtype),
            pltpu.VMEM((w3.shape[1], 3 * w3.shape[2]), w3.dtype),
            pltpu.SemaphoreType.DMA((7,)),
        ],
        compiler_params=pltpu.CompilerParams(vmem_limit_bytes=48 * 1024 * 1024),
    )(flags, xw, sk, pltpu.with_memory_space_constraint(wu, pltpu.HBM), bu, pltpu.with_memory_space_constraint(w3, pltpu.HBM), b3)


def shards(coarse, skip_field, up_weight, up_bias, conv_weight, conv_bias):
    peers = lax.axis_size("row")
    me = lax.axis_index("row")
    flags = jnp.stack([me == 0, me == peers - 1]).astype(jnp.int32)
    sk = skip_rows(skip_field, peers)
    xw = coarse_windows(coarse, peers)
    cout = up_weight.shape[3]
    wu = jnp.transpose(up_weight, (0, 1, 3, 2)).reshape(4, 4 * cout, -1)
    w3 = jnp.transpose(conv_weight, (0, 1, 3, 2)).reshape(3, 3 * cout, -1)
    return decode(flags, xw, sk, wu, up_bias[:, None], w3, conv_bias[:, None])


def solution(mesh):
    in_specs = (P("row", "member", None), P(None, ("member", "row"), None), P(), P(), P(), P())
    out_specs = P(None, ("member", "row"), None)
    return jax.shard_map(shards, mesh=mesh, in_specs=in_specs, out_specs=out_specs, check_vma=False)
```

```python
import jax
import jax.numpy as jnp
from jax import lax
from jax.experimental import pallas as pl
from jax.experimental.pallas import tpu as pltpu
from jax.sharding import PartitionSpec as P


def coarse_windows(coarse, peers):
    groups, rows, cols = coarse.shape
    tile = rows // peers
    padded = jnp.pad(coarse, ((0, 0), (1, tile - 1), (0, 0)))
    blocks = padded.reshape(groups, peers + 1, tile, cols)
    windows = jnp.concatenate([blocks[:, :peers], blocks[:, 1:, :2]], axis=2)
    windows = jnp.transpose(windows, (1, 2, 0, 3))
    gathered = lax.all_to_all(windows, "row", 0, 0, tiled=True)
    if groups % 8:
        gathered = jnp.transpose(gathered, (1, 0, 2, 3)).reshape(1, tile + 2, peers * groups, cols)
    return gathered


def skip_rows(skip, peers):
    up = [(i, i + 1) for i in range(peers - 1)]
    down = [(j, i) for i, j in up]
    before = lax.ppermute(skip[:, -1:], "row", up)
    after = lax.ppermute(skip[:, :1], "row", down)
    rimmed = jnp.concatenate([before, skip, after], axis=1)
    return jnp.transpose(rimmed, (1, 0, 2))


def lane_shift(v, period, step):
    lane = lax.broadcasted_iota(jnp.int32, v.shape, 1) % period
    edge = 0 if step > 0 else period - 1
    return jnp.where(lane == edge, 0.0, pltpu.roll(v, step % v.shape[1], 1))


def decoder_kernel(flags, xw_ref, sk_ref, wu_hbm, bu_ref, w3_hbm, b3_ref, out_ref, act_ref, wu_ref, w3_ref, sems):
    cin = wu_hbm.shape[2]

    def load(src, dst, k):
        copy = pltpu.make_async_copy(src, dst, sems.at[k])
        copy.start()
        return copy

    half = wu_hbm.shape[1] // 2
    up_loads = [
        [
            [load(wu_hbm.at[p + 2 * h, pl.ds(m * half, half)], wu_ref.at[p, pl.ds(m * half, half), pl.ds(h * cin, cin)], 4 * p + 2 * m + h) for h in range(2)]
            for m in range(2)
        ]
        for p in range(2)
    ]
    conv_loads = [load(w3_hbm.at[ky], w3_ref.at[:, pl.ds(ky * cin, cin)], 8 + ky) for ky in range(3)]
    peers, nwin, groups, cw = xw_ref.shape
    nfine, cout, fw = sk_ref.shape
    nout = nfine - 2
    span = (nwin - 1) * cw
    f32 = jnp.float32

    def dot(a, b):
        return jnp.dot(a, b, preferred_element_type=f32)

    def window_row(i):
        if peers == 1:
            return xw_ref[0, i]
        pieces = [xw_ref[s, i].astype(f32) for s in range(peers)]
        return jnp.concatenate(pieces, axis=0).astype(jnp.bfloat16)

    wide = jnp.concatenate([window_row(i) for i in range(nwin)], axis=1)
    stacked = jnp.concatenate([wide[:, cw:], wide[:, :span]], axis=0)
    parity = []
    for p in range(2):
        taps = []
        for m in range(2):
            for copy in up_loads[p][m]:
                copy.wait()
            z = dot(wu_ref[p, m * half : (m + 1) * half], stacked)
            taps += [z[k * cout : (k + 1) * cout] for k in range(2)]
        even = taps[1] + lane_shift(taps[3], cw, 1) + bu_ref[...]
        odd = taps[2] + lane_shift(taps[0], cw, -1) + bu_ref[...]
        parity.append((even.astype(jnp.bfloat16), odd.astype(jnp.bfloat16)))

    col = lax.broadcasted_iota(jnp.int32, (cw, fw), 0)
    pos = lax.broadcasted_iota(jnp.int32, (cw, fw), 1)
    put_even = (pos == 2 * col).astype(jnp.bfloat16)
    put_odd = (pos == 2 * col + 1).astype(jnp.bfloat16)
    put = jnp.concatenate([put_even, put_odd], axis=0)

    joined = []
    for t in range(nfine):
        even, odd = parity[t % 2]
        q = t // 2
        pair = jnp.concatenate([even[:, q * cw : (q + 1) * cw], odd[:, q * cw : (q + 1) * cw]], axis=1)
        row = dot(pair, put)
        if t == 0:
            row = jnp.where(flags[0] == 1, 0.0, row)
        if t == nfine - 1:
            row = jnp.where(flags[1] == 1, 0.0, row)
        joined.append(jnp.concatenate([sk_ref[t], row.astype(jnp.bfloat16)], axis=0))
    field = jnp.concatenate(joined, axis=1)
    for copy in conv_loads:
        copy.wait()

    rows = jnp.concatenate([field[:, ky * fw : (ky + nout) * fw] for ky in range(3)], axis=0)
    total = dot(w3_ref[...], rows)
    pre = total[cout : 2 * cout]
    pre = pre + lane_shift(total[:cout], fw, 1) + lane_shift(total[2 * cout :], fw, -1)
    pre = pre + b3_ref[...]
    act = pre / (1.0 + jnp.exp(-pre))
    for y in range(nout):
        act_ref[:, y, :] = act[:, y * fw : (y + 1) * fw]
    out_ref[...] = act_ref[...].astype(out_ref.dtype)


def decode(flags, xw, sk, wu, bu, w3, b3):
    nfine, cout, fw = sk.shape
    vmem = pl.BlockSpec(memory_space=pltpu.VMEM)
    hbm = pl.BlockSpec(memory_space=pltpu.HBM)
    return pl.pallas_call(
        decoder_kernel,
        out_shape=jax.ShapeDtypeStruct((cout, nfine - 2, fw), jnp.bfloat16),
        in_specs=[pl.BlockSpec(memory_space=pltpu.SMEM), vmem, vmem, hbm, vmem, hbm, vmem],
        out_specs=vmem,
        scratch_shapes=[
            pltpu.VMEM((cout, nfine - 2, fw), jnp.float32),
            pltpu.VMEM((2, wu.shape[1], 2 * wu.shape[2]), wu.dtype),
            pltpu.VMEM((w3.shape[1], 3 * w3.shape[2]), w3.dtype),
            pltpu.SemaphoreType.DMA((11,)),
        ],
        compiler_params=pltpu.CompilerParams(vmem_limit_bytes=48 * 1024 * 1024),
    )(flags, xw, sk, pltpu.with_memory_space_constraint(wu, pltpu.HBM), bu, pltpu.with_memory_space_constraint(w3, pltpu.HBM), b3)


def shards(coarse, skip_field, up_weight, up_bias, conv_weight, conv_bias):
    peers = lax.axis_size("row")
    me = lax.axis_index("row")
    flags = jnp.stack([me == 0, me == peers - 1]).astype(jnp.int32)
    sk = skip_rows(skip_field, peers)
    xw = coarse_windows(coarse, peers)
    cout = up_weight.shape[3]
    wu = jnp.transpose(up_weight, (0, 1, 3, 2)).reshape(4, 4 * cout, -1)
    w3 = jnp.transpose(conv_weight, (0, 1, 3, 2)).reshape(3, 3 * cout, -1)
    return decode(flags, xw, sk, wu, up_bias[:, None], w3, conv_bias[:, None])


def solution(mesh):
    in_specs = (P("row", "member", None), P(None, ("member", "row"), None), P(), P(), P(), P())
    out_specs = P(None, ("member", "row"), None)
    return jax.shard_map(shards, mesh=mesh, in_specs=in_specs, out_specs=out_specs, check_vma=False)
```

```python
import jax
import jax.numpy as jnp
from jax import lax
from jax.experimental import pallas as pl
from jax.experimental.pallas import tpu as pltpu
from jax.sharding import PartitionSpec as P


def coarse_windows(coarse, peers):
    groups, rows, cols = coarse.shape
    tile = rows // peers
    padded = jnp.pad(coarse, ((0, 0), (1, tile - 1), (0, 0)))
    blocks = padded.reshape(groups, peers + 1, tile, cols)
    windows = jnp.concatenate([blocks[:, :peers], blocks[:, 1:, :2]], axis=2)
    windows = jnp.transpose(windows, (1, 2, 0, 3))
    gathered = lax.all_to_all(windows, "row", 0, 0, tiled=True)
    if groups % 8:
        gathered = jnp.transpose(gathered, (1, 0, 2, 3)).reshape(1, tile + 2, peers * groups, cols)
    return gathered


def skip_rows(skip, peers):
    up = [(i, i + 1) for i in range(peers - 1)]
    down = [(j, i) for i, j in up]
    before = lax.ppermute(skip[:, -1:], "row", up)
    after = lax.ppermute(skip[:, :1], "row", down)
    rimmed = jnp.concatenate([before, skip, after], axis=1)
    return jnp.transpose(rimmed, (1, 0, 2))


def lane_shift(v, period, step):
    lane = lax.broadcasted_iota(jnp.int32, v.shape, 1) % period
    edge = 0 if step > 0 else period - 1
    return jnp.where(lane == edge, 0.0, pltpu.roll(v, step % v.shape[1], 1))


def decoder_kernel(flags, xw_ref, sk_ref, wu_hbm, bu_ref, w3_hbm, b3_ref, out_ref, act_ref, wu_ref, w3_ref, sems):
    cin = wu_hbm.shape[2]

    def load(src, dst, k):
        copy = pltpu.make_async_copy(src, dst, sems.at[k])
        copy.start()
        return copy

    up_loads = [[load(wu_hbm.at[p + 2 * h], wu_ref.at[p, :, pl.ds(h * cin, cin)], 2 * p + h) for h in range(2)] for p in range(2)]
    conv_loads = [load(w3_hbm.at[ky], w3_ref.at[:, pl.ds(ky * cin, cin)], 4 + ky) for ky in range(3)]
    peers, nwin, groups, cw = xw_ref.shape
    nfine, cout, fw = sk_ref.shape
    nout = nfine - 2
    span = (nwin - 1) * cw
    f32 = jnp.float32

    def dot(a, b):
        return jnp.dot(a, b, preferred_element_type=f32)

    def window_row(i):
        if peers == 1:
            return xw_ref[0, i]
        pieces = [xw_ref[s, i].astype(f32) for s in range(peers)]
        return jnp.concatenate(pieces, axis=0).astype(jnp.bfloat16)

    wide = jnp.concatenate([window_row(i) for i in range(nwin)], axis=1)
    stacked = jnp.concatenate([wide[:, cw:], wide[:, :span]], axis=0)
    parity = []
    for p in range(2):
        for copy in up_loads[p]:
            copy.wait()
        z = dot(wu_ref[p], stacked)
        taps = [z[k * cout : (k + 1) * cout] for k in range(4)]
        even = taps[1] + lane_shift(taps[3], cw, 1) + bu_ref[...]
        odd = taps[2] + lane_shift(taps[0], cw, -1) + bu_ref[...]
        parity.append((even.astype(jnp.bfloat16), odd.astype(jnp.bfloat16)))

    col = lax.broadcasted_iota(jnp.int32, (cw, fw), 0)
    pos = lax.broadcasted_iota(jnp.int32, (cw, fw), 1)
    put_even = (pos == 2 * col).astype(jnp.bfloat16)
    put_odd = (pos == 2 * col + 1).astype(jnp.bfloat16)
    put = jnp.concatenate([put_even, put_odd], axis=0)

    joined = []
    for t in range(nfine):
        even, odd = parity[t % 2]
        q = t // 2
        pair = jnp.concatenate([even[:, q * cw : (q + 1) * cw], odd[:, q * cw : (q + 1) * cw]], axis=1)
        row = dot(pair, put)
        if t == 0:
            row = jnp.where(flags[0] == 1, 0.0, row)
        if t == nfine - 1:
            row = jnp.where(flags[1] == 1, 0.0, row)
        joined.append(jnp.concatenate([sk_ref[t], row.astype(jnp.bfloat16)], axis=0))
    for copy in conv_loads:
        copy.wait()

    rows = jnp.concatenate([jnp.concatenate(joined[ky : ky + nout], axis=1) for ky in range(3)], axis=0)
    total = dot(w3_ref[...], rows)
    pre = total[cout : 2 * cout]
    pre = pre + lane_shift(total[:cout], fw, 1) + lane_shift(total[2 * cout :], fw, -1)
    pre = pre + b3_ref[...]
    act = pre / (1.0 + jnp.exp(-pre))
    for y in range(nout):
        act_ref[:, y, :] = act[:, y * fw : (y + 1) * fw]
    out_ref[...] = act_ref[...].astype(out_ref.dtype)


def decode(flags, xw, sk, wu, bu, w3, b3):
    nfine, cout, fw = sk.shape
    vmem = pl.BlockSpec(memory_space=pltpu.VMEM)
    hbm = pl.BlockSpec(memory_space=pltpu.HBM)
    return pl.pallas_call(
        decoder_kernel,
        out_shape=jax.ShapeDtypeStruct((cout, nfine - 2, fw), jnp.bfloat16),
        in_specs=[pl.BlockSpec(memory_space=pltpu.SMEM), vmem, vmem, hbm, vmem, hbm, vmem],
        out_specs=vmem,
        scratch_shapes=[
            pltpu.VMEM((cout, nfine - 2, fw), jnp.float32),
            pltpu.VMEM((2, wu.shape[1], 2 * wu.shape[2]), wu.dtype),
            pltpu.VMEM((w3.shape[1], 3 * w3.shape[2]), w3.dtype),
            pltpu.SemaphoreType.DMA((7,)),
        ],
        compiler_params=pltpu.CompilerParams(vmem_limit_bytes=48 * 1024 * 1024),
    )(flags, xw, sk, pltpu.with_memory_space_constraint(wu, pltpu.HBM), bu, pltpu.with_memory_space_constraint(w3, pltpu.HBM), b3)


def shards(coarse, skip_field, up_weight, up_bias, conv_weight, conv_bias):
    peers = lax.axis_size("row")
    me = lax.axis_index("row")
    flags = jnp.stack([me == 0, me == peers - 1]).astype(jnp.int32)
    sk = skip_rows(skip_field, peers)
    xw = coarse_windows(coarse, peers)
    cout = up_weight.shape[3]
    wu = jnp.transpose(up_weight, (0, 1, 3, 2)).reshape(4, 4 * cout, -1)
    w3 = jnp.transpose(conv_weight, (0, 1, 3, 2)).reshape(3, 3 * cout, -1)
    return decode(flags, xw, sk, wu, up_bias[:, None], w3, conv_bias[:, None])


def solution(mesh):
    in_specs = (P("row", "member", None), P(None, ("member", "row"), None), P(), P(), P(), P())
    out_specs = P(None, ("member", "row"), None)
    return jax.shard_map(shards, mesh=mesh, in_specs=in_specs, out_specs=out_specs, check_vma=False)
```

```python
import jax
import jax.numpy as jnp
from jax import lax
from jax.experimental import pallas as pl
from jax.experimental.pallas import tpu as pltpu
from jax.sharding import PartitionSpec as P


def coarse_windows(coarse, peers):
    groups, rows, cols = coarse.shape
    tile = rows // peers
    padded = jnp.pad(coarse, ((0, 0), (1, tile - 1), (0, 0)))
    blocks = padded.reshape(groups, peers + 1, tile, cols)
    windows = jnp.concatenate([blocks[:, :peers], blocks[:, 1:, :2]], axis=2)
    windows = jnp.transpose(windows, (1, 2, 0, 3))
    gathered = lax.all_to_all(windows, "row", 0, 0, tiled=True)
    if groups % 8:
        gathered = jnp.transpose(gathered, (1, 0, 2, 3)).reshape(1, tile + 2, peers * groups, cols)
    return gathered


def skip_rows(skip, peers):
    up = [(i, i + 1) for i in range(peers - 1)]
    down = [(j, i) for i, j in up]
    before = lax.ppermute(skip[:, -1:], "row", up)
    after = lax.ppermute(skip[:, :1], "row", down)
    rimmed = jnp.concatenate([before, skip, after], axis=1)
    return jnp.transpose(rimmed, (1, 0, 2))


def lane_shift(v, period, step):
    lane = lax.broadcasted_iota(jnp.int32, v.shape, 1) % period
    edge = 0 if step > 0 else period - 1
    return jnp.where(lane == edge, 0.0, pltpu.roll(v, step % v.shape[1], 1))


def decoder_kernel(flags, xw_ref, sk_ref, wu_hbm, bu_ref, w3_hbm, b3_ref, out_ref, act_ref, wu_ref, w3_ref, sems):
    cin = wu_hbm.shape[2]

    def load(src, dst, k):
        copy = pltpu.make_async_copy(src, dst, sems.at[k])
        copy.start()
        return copy

    up_loads = [[load(wu_hbm.at[p + 2 * h], wu_ref.at[p, :, pl.ds(h * cin, cin)], 2 * p + h) for h in range(2)] for p in range(2)]
    conv_loads = [load(w3_hbm.at[ky], w3_ref.at[:, pl.ds(ky * cin, cin)], 4 + ky) for ky in range(3)]
    peers, nwin, groups, cw = xw_ref.shape
    nfine, cout, fw = sk_ref.shape
    nout = nfine - 2
    span = (nwin - 1) * cw
    f32 = jnp.float32

    def dot(a, b):
        return jnp.dot(a, b, preferred_element_type=f32)

    def window_row(i):
        if peers == 1:
            return xw_ref[0, i]
        pieces = [xw_ref[s, i].astype(f32) for s in range(peers)]
        return jnp.concatenate(pieces, axis=0).astype(jnp.bfloat16)

    wide = jnp.concatenate([window_row(i) for i in range(nwin)], axis=1)
    stacked = jnp.concatenate([wide[:, cw:], wide[:, :span]], axis=0)
    parity = []
    for p in range(2):
        for copy in up_loads[p]:
            copy.wait()
        z = dot(wu_ref[p], stacked)
        taps = [z[k * cout : (k + 1) * cout] for k in range(4)]
        even = taps[1] + lane_shift(taps[3], cw, 1) + bu_ref[...]
        odd = taps[2] + lane_shift(taps[0], cw, -1) + bu_ref[...]
        parity.append((even.astype(jnp.bfloat16), odd.astype(jnp.bfloat16)))

    col = lax.broadcasted_iota(jnp.int32, (cw, fw), 0)
    pos = lax.broadcasted_iota(jnp.int32, (cw, fw), 1)
    put_even = (pos == 2 * col).astype(jnp.bfloat16)
    put_odd = (pos == 2 * col + 1).astype(jnp.bfloat16)
    put = jnp.concatenate([put_even, put_odd], axis=0)

    pairs = []
    for t in range(nfine):
        even, odd = parity[t % 2]
        q = t // 2
        pairs.append(jnp.concatenate([even[:, q * cw : (q + 1) * cw], odd[:, q * cw : (q + 1) * cw]], axis=1))
    placed = dot(jnp.concatenate(pairs, axis=0), put)

    joined = []
    for t in range(nfine):
        row = placed[t * cout : (t + 1) * cout]
        if t == 0:
            row = jnp.where(flags[0] == 1, 0.0, row)
        if t == nfine - 1:
            row = jnp.where(flags[1] == 1, 0.0, row)
        joined.append(jnp.concatenate([sk_ref[t], row.astype(jnp.bfloat16)], axis=0))
    field = jnp.concatenate(joined, axis=1)
    for copy in conv_loads:
        copy.wait()

    rows = jnp.concatenate([field[:, ky * fw : (ky + nout) * fw] for ky in range(3)], axis=0)
    total = dot(w3_ref[...], rows)
    pre = total[cout : 2 * cout]
    pre = pre + lane_shift(total[:cout], fw, 1) + lane_shift(total[2 * cout :], fw, -1)
    pre = pre + b3_ref[...]
    act = pre / (1.0 + jnp.exp(-pre))
    for y in range(nout):
        act_ref[:, y, :] = act[:, y * fw : (y + 1) * fw]
    out_ref[...] = act_ref[...].astype(out_ref.dtype)


def decode(flags, xw, sk, wu, bu, w3, b3):
    nfine, cout, fw = sk.shape
    vmem = pl.BlockSpec(memory_space=pltpu.VMEM)
    hbm = pl.BlockSpec(memory_space=pltpu.HBM)
    return pl.pallas_call(
        decoder_kernel,
        out_shape=jax.ShapeDtypeStruct((cout, nfine - 2, fw), jnp.bfloat16),
        in_specs=[pl.BlockSpec(memory_space=pltpu.SMEM), vmem, vmem, hbm, vmem, hbm, vmem],
        out_specs=vmem,
        scratch_shapes=[
            pltpu.VMEM((cout, nfine - 2, fw), jnp.float32),
            pltpu.VMEM((2, wu.shape[1], 2 * wu.shape[2]), wu.dtype),
            pltpu.VMEM((w3.shape[1], 3 * w3.shape[2]), w3.dtype),
            pltpu.SemaphoreType.DMA((7,)),
        ],
        compiler_params=pltpu.CompilerParams(vmem_limit_bytes=48 * 1024 * 1024),
    )(flags, xw, sk, pltpu.with_memory_space_constraint(wu, pltpu.HBM), bu, pltpu.with_memory_space_constraint(w3, pltpu.HBM), b3)


def shards(coarse, skip_field, up_weight, up_bias, conv_weight, conv_bias):
    peers = lax.axis_size("row")
    me = lax.axis_index("row")
    flags = jnp.stack([me == 0, me == peers - 1]).astype(jnp.int32)
    sk = skip_rows(skip_field, peers)
    xw = coarse_windows(coarse, peers)
    cout = up_weight.shape[3]
    wu = jnp.transpose(up_weight, (0, 1, 3, 2)).reshape(4, 4 * cout, -1)
    w3 = jnp.transpose(conv_weight, (0, 1, 3, 2)).reshape(3, 3 * cout, -1)
    return decode(flags, xw, sk, wu, up_bias[:, None], w3, conv_bias[:, None])


def solution(mesh):
    in_specs = (P("row", "member", None), P(None, ("member", "row"), None), P(), P(), P(), P())
    out_specs = P(None, ("member", "row"), None)
    return jax.shard_map(shards, mesh=mesh, in_specs=in_specs, out_specs=out_specs, check_vma=False)
```

```python
import jax
import jax.numpy as jnp
from jax import lax
from jax.experimental import pallas as pl
from jax.experimental.pallas import tpu as pltpu
from jax.sharding import PartitionSpec as P


def coarse_windows(coarse, peers):
    groups, rows, cols = coarse.shape
    tile = rows // peers
    padded = jnp.pad(coarse, ((0, 0), (1, tile - 1), (0, 0)))
    blocks = padded.reshape(groups, peers + 1, tile, cols)
    windows = jnp.concatenate([blocks[:, :peers], blocks[:, 1:, :2]], axis=2)
    windows = jnp.transpose(windows, (1, 2, 0, 3))
    gathered = lax.all_to_all(windows, "row", 0, 0, tiled=True)
    if groups % 8:
        gathered = jnp.transpose(gathered, (1, 0, 2, 3)).reshape(1, tile + 2, peers * groups, cols)
    return gathered


def skip_rows(skip, peers):
    up = [(i, i + 1) for i in range(peers - 1)]
    down = [(j, i) for i, j in up]
    before = lax.ppermute(skip[:, -1:], "row", up)
    after = lax.ppermute(skip[:, :1], "row", down)
    rimmed = jnp.concatenate([before, skip, after], axis=1)
    return jnp.transpose(rimmed, (1, 0, 2))


def lane_shift(v, period, step):
    lane = lax.broadcasted_iota(jnp.int32, v.shape, 1) % period
    edge = 0 if step > 0 else period - 1
    return jnp.where(lane == edge, 0.0, pltpu.roll(v, step % v.shape[1], 1))


def decoder_kernel(flags, xw_ref, sk_ref, wu_hbm, bu_ref, w3_hbm, b3_ref, out_ref, act_ref, out_buf, wu_ref, w3_ref, sems):
    cin = wu_hbm.shape[2]

    def load(src, dst, k):
        copy = pltpu.make_async_copy(src, dst, sems.at[k])
        copy.start()
        return copy

    up_loads = [[load(wu_hbm.at[p + 2 * h], wu_ref.at[p, :, pl.ds(h * cin, cin)], 2 * p + h) for h in range(2)] for p in range(2)]
    conv_loads = [load(w3_hbm.at[ky], w3_ref.at[:, pl.ds(ky * cin, cin)], 4 + ky) for ky in range(3)]
    peers, nwin, groups, cw = xw_ref.shape
    nfine, cout, fw = sk_ref.shape
    nout = nfine - 2
    span = (nwin - 1) * cw
    f32 = jnp.float32

    def dot(a, b):
        return jnp.dot(a, b, preferred_element_type=f32)

    def window_row(i):
        if peers == 1:
            return xw_ref[0, i]
        pieces = [xw_ref[s, i].astype(f32) for s in range(peers)]
        return jnp.concatenate(pieces, axis=0).astype(jnp.bfloat16)

    wide = jnp.concatenate([window_row(i) for i in range(nwin)], axis=1)
    stacked = jnp.concatenate([wide[:, cw:], wide[:, :span]], axis=0)
    parity = []
    for p in range(2):
        for copy in up_loads[p]:
            copy.wait()
        z = dot(wu_ref[p], stacked)
        taps = [z[k * cout : (k + 1) * cout] for k in range(4)]
        even = taps[1] + lane_shift(taps[3], cw, 1) + bu_ref[...]
        odd = taps[2] + lane_shift(taps[0], cw, -1) + bu_ref[...]
        parity.append((even.astype(jnp.bfloat16), odd.astype(jnp.bfloat16)))

    col = lax.broadcasted_iota(jnp.int32, (cw, fw), 0)
    pos = lax.broadcasted_iota(jnp.int32, (cw, fw), 1)
    put_even = (pos == 2 * col).astype(jnp.bfloat16)
    put_odd = (pos == 2 * col + 1).astype(jnp.bfloat16)
    put = jnp.concatenate([put_even, put_odd], axis=0)

    joined = []
    for t in range(nfine):
        even, odd = parity[t % 2]
        q = t // 2
        pair = jnp.concatenate([even[:, q * cw : (q + 1) * cw], odd[:, q * cw : (q + 1) * cw]], axis=1)
        row = dot(pair, put)
        if t == 0:
            row = jnp.where(flags[0] == 1, 0.0, row)
        if t == nfine - 1:
            row = jnp.where(flags[1] == 1, 0.0, row)
        joined.append(jnp.concatenate([sk_ref[t], row.astype(jnp.bfloat16)], axis=0))
    field = jnp.concatenate(joined, axis=1)
    for copy in conv_loads:
        copy.wait()

    rows = jnp.concatenate([field[:, ky * fw : (ky + nout) * fw] for ky in range(3)], axis=0)
    total = dot(w3_ref[...], rows)
    block = cout // 3 if cout % 48 == 0 else cout
    stores = []
    for c0 in range(0, cout, block):
        part = lambda kx: total[kx * cout + c0 : kx * cout + c0 + block]
        pre = part(1) + lane_shift(part(0), fw, 1) + lane_shift(part(2), fw, -1)
        pre = pre + b3_ref[pl.ds(c0, block)]
        act = pre / (1.0 + jnp.exp(-pre))
        for y in range(nout):
            act_ref[pl.ds(c0, block), y, :] = act[:, y * fw : (y + 1) * fw]
        out_buf[pl.ds(c0, block)] = act_ref[pl.ds(c0, block)].astype(out_buf.dtype)
        stores.append(load(out_buf.at[pl.ds(c0, block)], out_ref.at[pl.ds(c0, block)], 7 + len(stores)))
    for copy in stores:
        copy.wait()


def decode(flags, xw, sk, wu, bu, w3, b3):
    nfine, cout, fw = sk.shape
    vmem = pl.BlockSpec(memory_space=pltpu.VMEM)
    hbm = pl.BlockSpec(memory_space=pltpu.HBM)
    return pl.pallas_call(
        decoder_kernel,
        out_shape=jax.ShapeDtypeStruct((cout, nfine - 2, fw), jnp.bfloat16),
        in_specs=[pl.BlockSpec(memory_space=pltpu.SMEM), vmem, vmem, hbm, vmem, hbm, vmem],
        out_specs=pl.BlockSpec(memory_space=pl.ANY),
        scratch_shapes=[
            pltpu.VMEM((cout, nfine - 2, fw), jnp.float32),
            pltpu.VMEM((cout, nfine - 2, fw), jnp.bfloat16),
            pltpu.VMEM((2, wu.shape[1], 2 * wu.shape[2]), wu.dtype),
            pltpu.VMEM((w3.shape[1], 3 * w3.shape[2]), w3.dtype),
            pltpu.SemaphoreType.DMA((10,)),
        ],
        compiler_params=pltpu.CompilerParams(vmem_limit_bytes=48 * 1024 * 1024),
    )(flags, xw, sk, pltpu.with_memory_space_constraint(wu, pltpu.HBM), bu, pltpu.with_memory_space_constraint(w3, pltpu.HBM), b3)


def shards(coarse, skip_field, up_weight, up_bias, conv_weight, conv_bias):
    peers = lax.axis_size("row")
    me = lax.axis_index("row")
    flags = jnp.stack([me == 0, me == peers - 1]).astype(jnp.int32)
    sk = skip_rows(skip_field, peers)
    xw = coarse_windows(coarse, peers)
    cout = up_weight.shape[3]
    wu = jnp.transpose(up_weight, (0, 1, 3, 2)).reshape(4, 4 * cout, -1)
    w3 = jnp.transpose(conv_weight, (0, 1, 3, 2)).reshape(3, 3 * cout, -1)
    return decode(flags, xw, sk, wu, up_bias[:, None], w3, conv_bias[:, None])


def solution(mesh):
    in_specs = (P("row", "member", None), P(None, ("member", "row"), None), P(), P(), P(), P())
    out_specs = P(None, ("member", "row"), None)
    return jax.shard_map(shards, mesh=mesh, in_specs=in_specs, out_specs=out_specs, check_vma=False)
```

```python
import jax
import jax.numpy as jnp
from jax import lax
from jax.experimental import pallas as pl
from jax.experimental.pallas import tpu as pltpu
from jax.sharding import PartitionSpec as P


def coarse_windows(coarse, peers):
    groups, rows, cols = coarse.shape
    tile = rows // peers
    padded = jnp.pad(coarse, ((0, 0), (1, tile - 1), (0, 0)))
    blocks = padded.reshape(groups, peers + 1, tile, cols)
    windows = jnp.concatenate([blocks[:, :peers], blocks[:, 1:, :2]], axis=2)
    windows = jnp.transpose(windows, (1, 2, 0, 3))
    gathered = lax.all_to_all(windows, "row", 0, 0, tiled=True)
    if groups % 8:
        gathered = jnp.transpose(gathered, (1, 0, 2, 3)).reshape(1, tile + 2, peers * groups, cols)
    return gathered


def skip_rows(skip, peers):
    up = [(i, i + 1) for i in range(peers - 1)]
    down = [(j, i) for i, j in up]
    before = lax.ppermute(skip[:, -1:], "row", up)
    after = lax.ppermute(skip[:, :1], "row", down)
    rimmed = jnp.concatenate([before, skip, after], axis=1)
    return jnp.transpose(rimmed, (1, 0, 2))


def lane_shift(v, period, step):
    lane = lax.broadcasted_iota(jnp.int32, v.shape, 1) % period
    edge = 0 if step > 0 else period - 1
    return jnp.where(lane == edge, 0.0, pltpu.roll(v, step % v.shape[1], 1))


def decoder_kernel(flags, xw_ref, sk_ref, wu_hbm, bu_ref, w3_hbm, b3_ref, out_ref, act_ref, wu_ref, w3_ref, sems):
    cin = wu_hbm.shape[2]

    def load(src, dst, k):
        copy = pltpu.make_async_copy(src, dst, sems.at[k])
        copy.start()
        return copy

    up_loads = [[load(wu_hbm.at[p + 2 * h], wu_ref.at[p, :, pl.ds(h * cin, cin)], 2 * p + h) for h in range(2)] for p in range(2)]
    conv_loads = [load(w3_hbm.at[ky], w3_ref.at[:, pl.ds(ky * cin, cin)], 4 + ky) for ky in range(3)]
    peers, nwin, groups, cw = xw_ref.shape
    nfine, cout, fw = sk_ref.shape
    nout = nfine - 2
    span = (nwin - 1) * cw
    f32 = jnp.float32

    def dot(a, b):
        return jnp.dot(a, b, preferred_element_type=f32)

    def window_row(i):
        if peers == 1:
            return xw_ref[0, i]
        pieces = [xw_ref[s, i].astype(f32) for s in range(peers)]
        return jnp.concatenate(pieces, axis=0).astype(jnp.bfloat16)

    wide = jnp.concatenate([window_row(i) for i in range(nwin)], axis=1)
    stacked = jnp.concatenate([wide[:, cw:], wide[:, :span]], axis=0)
    for copies in up_loads:
        for copy in copies:
            copy.wait()
    zz = dot(wu_ref[...].reshape(2 * wu_ref.shape[1], wu_ref.shape[2]), stacked)
    parity = []
    for p in range(2):
        z = zz[p * 4 * cout : (p + 1) * 4 * cout]
        taps = [z[k * cout : (k + 1) * cout] for k in range(4)]
        even = taps[1] + lane_shift(taps[3], cw, 1) + bu_ref[...]
        odd = taps[2] + lane_shift(taps[0], cw, -1) + bu_ref[...]
        parity.append((even.astype(jnp.bfloat16), odd.astype(jnp.bfloat16)))

    col = lax.broadcasted_iota(jnp.int32, (cw, fw), 0)
    pos = lax.broadcasted_iota(jnp.int32, (cw, fw), 1)
    put_even = (pos == 2 * col).astype(jnp.bfloat16)
    put_odd = (pos == 2 * col + 1).astype(jnp.bfloat16)
    put = jnp.concatenate([put_even, put_odd], axis=0)

    joined = []
    for t in range(nfine):
        even, odd = parity[t % 2]
        q = t // 2
        pair = jnp.concatenate([even[:, q * cw : (q + 1) * cw], odd[:, q * cw : (q + 1) * cw]], axis=1)
        row = dot(pair, put)
        if t == 0:
            row = jnp.where(flags[0] == 1, 0.0, row)
        if t == nfine - 1:
            row = jnp.where(flags[1] == 1, 0.0, row)
        joined.append(jnp.concatenate([sk_ref[t], row.astype(jnp.bfloat16)], axis=0))
    field = jnp.concatenate(joined, axis=1)
    for copy in conv_loads:
        copy.wait()

    rows = jnp.concatenate([field[:, ky * fw : (ky + nout) * fw] for ky in range(3)], axis=0)
    total = dot(w3_ref[...], rows)
    pre = total[cout : 2 * cout]
    pre = pre + lane_shift(total[:cout], fw, 1) + lane_shift(total[2 * cout :], fw, -1)
    pre = pre + b3_ref[...]
    act = pre / (1.0 + jnp.exp(-pre))
    for y in range(nout):
        act_ref[:, y, :] = act[:, y * fw : (y + 1) * fw]
    out_ref[...] = act_ref[...].astype(out_ref.dtype)


def decode(flags, xw, sk, wu, bu, w3, b3):
    nfine, cout, fw = sk.shape
    vmem = pl.BlockSpec(memory_space=pltpu.VMEM)
    hbm = pl.BlockSpec(memory_space=pltpu.HBM)
    return pl.pallas_call(
        decoder_kernel,
        out_shape=jax.ShapeDtypeStruct((cout, nfine - 2, fw), jnp.bfloat16),
        in_specs=[pl.BlockSpec(memory_space=pltpu.SMEM), vmem, vmem, hbm, vmem, hbm, vmem],
        out_specs=vmem,
        scratch_shapes=[
            pltpu.VMEM((cout, nfine - 2, fw), jnp.float32),
            pltpu.VMEM((2, wu.shape[1], 2 * wu.shape[2]), wu.dtype),
            pltpu.VMEM((w3.shape[1], 3 * w3.shape[2]), w3.dtype),
            pltpu.SemaphoreType.DMA((7,)),
        ],
        compiler_params=pltpu.CompilerParams(vmem_limit_bytes=48 * 1024 * 1024),
    )(flags, xw, sk, pltpu.with_memory_space_constraint(wu, pltpu.HBM), bu, pltpu.with_memory_space_constraint(w3, pltpu.HBM), b3)


def shards(coarse, skip_field, up_weight, up_bias, conv_weight, conv_bias):
    peers = lax.axis_size("row")
    me = lax.axis_index("row")
    flags = jnp.stack([me == 0, me == peers - 1]).astype(jnp.int32)
    sk = skip_rows(skip_field, peers)
    xw = coarse_windows(coarse, peers)
    cout = up_weight.shape[3]
    wu = jnp.transpose(up_weight, (0, 1, 3, 2)).reshape(4, 4 * cout, -1)
    w3 = jnp.transpose(conv_weight, (0, 1, 3, 2)).reshape(3, 3 * cout, -1)
    return decode(flags, xw, sk, wu, up_bias[:, None], w3, conv_bias[:, None])


def solution(mesh):
    in_specs = (P("row", "member", None), P(None, ("member", "row"), None), P(), P(), P(), P())
    out_specs = P(None, ("member", "row"), None)
    return jax.shard_map(shards, mesh=mesh, in_specs=in_specs, out_specs=out_specs, check_vma=False)
```

```python
import jax
import jax.numpy as jnp
from jax import lax
from jax.experimental import pallas as pl
from jax.experimental.pallas import tpu as pltpu
from jax.sharding import PartitionSpec as P


def coarse_windows(coarse, peers):
    groups, rows, cols = coarse.shape
    tile = rows // peers
    padded = jnp.pad(coarse, ((0, 0), (1, tile - 1), (0, 0)))
    blocks = padded.reshape(groups, peers + 1, tile, cols)
    windows = jnp.concatenate([blocks[:, :peers], blocks[:, 1:, :2]], axis=2)
    windows = jnp.transpose(windows, (1, 2, 0, 3))
    gathered = lax.all_to_all(windows, "row", 0, 0, tiled=True)
    if groups % 8:
        gathered = jnp.transpose(gathered, (1, 0, 2, 3)).reshape(1, tile + 2, peers * groups, cols)
    return gathered


def skip_rows(skip, peers):
    up = [(i, i + 1) for i in range(peers - 1)]
    down = [(j, i) for i, j in up]
    before = lax.ppermute(skip[:, -1:], "row", up)
    after = lax.ppermute(skip[:, :1], "row", down)
    rimmed = jnp.concatenate([before, skip, after], axis=1)
    return jnp.transpose(rimmed, (1, 0, 2))


def lane_shift(v, period, step):
    lane = lax.broadcasted_iota(jnp.int32, v.shape, 1) % period
    edge = 0 if step > 0 else period - 1
    return jnp.where(lane == edge, 0.0, pltpu.roll(v, step % v.shape[1], 1))


def decoder_kernel(flags, xw_ref, sk_ref, wu_hbm, bu_ref, w3_hbm, b3_ref, out_ref, act_ref, wu_ref, w3_ref, sems):
    cin = wu_hbm.shape[2]

    def load(src, dst, k):
        copy = pltpu.make_async_copy(src, dst, sems.at[k])
        copy.start()
        return copy

    up_loads = [[load(wu_hbm.at[p + 2 * h], wu_ref.at[p, :, pl.ds(h * cin, cin)], 2 * p + h) for h in range(2)] for p in range(2)]
    conv_loads = [load(w3_hbm.at[ky], w3_ref.at[:, pl.ds(ky * cin, cin)], 4 + ky) for ky in range(3)]
    peers, nwin, groups, cw = xw_ref.shape
    nfine, cout, fw = sk_ref.shape
    nout = nfine - 2
    span = (nwin - 1) * cw
    f32 = jnp.float32

    def dot(a, b):
        return jnp.dot(a, b, preferred_element_type=f32)

    def window_row(i):
        if peers == 1:
            return xw_ref[0, i]
        pieces = [xw_ref[s, i].astype(f32) for s in range(peers)]
        return jnp.concatenate(pieces, axis=0).astype(jnp.bfloat16)

    wide = jnp.concatenate([window_row(i) for i in range(nwin)], axis=1)
    stacked = jnp.concatenate([wide[:, cw:], wide[:, :span]], axis=0)
    parity = []
    for p in range(2):
        for copy in up_loads[p]:
            copy.wait()
        z = dot(wu_ref[p], stacked)
        taps = [z[k * cout : (k + 1) * cout] for k in range(4)]
        even = taps[1] + lane_shift(taps[3], cw, 1) + bu_ref[...]
        odd = taps[2] + lane_shift(taps[0], cw, -1) + bu_ref[...]
        parity.append((even.astype(jnp.bfloat16), odd.astype(jnp.bfloat16)))

    col = lax.broadcasted_iota(jnp.int32, (cw, fw), 0)
    pos = lax.broadcasted_iota(jnp.int32, (cw, fw), 1)
    put_even = (pos == 2 * col).astype(jnp.bfloat16)
    put_odd = (pos == 2 * col + 1).astype(jnp.bfloat16)
    put = jnp.concatenate([put_even, put_odd], axis=0)

    joined = []
    for t in range(nfine):
        even, odd = parity[t % 2]
        q = t // 2
        pair = jnp.concatenate([even[:, q * cw : (q + 1) * cw], odd[:, q * cw : (q + 1) * cw]], axis=1)
        row = dot(pair, put)
        if t == 0:
            row = jnp.where(flags[0] == 1, 0.0, row)
        if t == nfine - 1:
            row = jnp.where(flags[1] == 1, 0.0, row)
        joined.append(jnp.concatenate([sk_ref[t], row.astype(jnp.bfloat16)], axis=0))
    field = jnp.concatenate(joined, axis=1)
    for copy in conv_loads:
        copy.wait()

    step = 2 if nout % 2 == 0 else 1
    for y0 in range(0, nout, step):
        rows = jnp.concatenate([field[:, (y0 + ky) * fw : (y0 + ky + step) * fw] for ky in range(3)], axis=0)
        total = dot(w3_ref[...], rows)
        pre = total[cout : 2 * cout]
        pre = pre + lane_shift(total[:cout], fw, 1) + lane_shift(total[2 * cout :], fw, -1)
        pre = pre + b3_ref[...]
        act = pre / (1.0 + jnp.exp(-pre))
        for i in range(step):
            act_ref[:, y0 + i, :] = act[:, i * fw : (i + 1) * fw]
    out_ref[...] = act_ref[...].astype(out_ref.dtype)


def decode(flags, xw, sk, wu, bu, w3, b3):
    nfine, cout, fw = sk.shape
    vmem = pl.BlockSpec(memory_space=pltpu.VMEM)
    hbm = pl.BlockSpec(memory_space=pltpu.HBM)
    return pl.pallas_call(
        decoder_kernel,
        out_shape=jax.ShapeDtypeStruct((cout, nfine - 2, fw), jnp.bfloat16),
        in_specs=[pl.BlockSpec(memory_space=pltpu.SMEM), vmem, vmem, hbm, vmem, hbm, vmem],
        out_specs=vmem,
        scratch_shapes=[
            pltpu.VMEM((cout, nfine - 2, fw), jnp.float32),
            pltpu.VMEM((2, wu.shape[1], 2 * wu.shape[2]), wu.dtype),
            pltpu.VMEM((w3.shape[1], 3 * w3.shape[2]), w3.dtype),
            pltpu.SemaphoreType.DMA((7,)),
        ],
        compiler_params=pltpu.CompilerParams(vmem_limit_bytes=48 * 1024 * 1024),
    )(flags, xw, sk, pltpu.with_memory_space_constraint(wu, pltpu.HBM), bu, pltpu.with_memory_space_constraint(w3, pltpu.HBM), b3)


def shards(coarse, skip_field, up_weight, up_bias, conv_weight, conv_bias):
    peers = lax.axis_size("row")
    me = lax.axis_index("row")
    flags = jnp.stack([me == 0, me == peers - 1]).astype(jnp.int32)
    sk = skip_rows(skip_field, peers)
    xw = coarse_windows(coarse, peers)
    cout = up_weight.shape[3]
    wu = jnp.transpose(up_weight, (0, 1, 3, 2)).reshape(4, 4 * cout, -1)
    w3 = jnp.transpose(conv_weight, (0, 1, 3, 2)).reshape(3, 3 * cout, -1)
    return decode(flags, xw, sk, wu, up_bias[:, None], w3, conv_bias[:, None])


def solution(mesh):
    in_specs = (P("row", "member", None), P(None, ("member", "row"), None), P(), P(), P(), P())
    out_specs = P(None, ("member", "row"), None)
    return jax.shard_map(shards, mesh=mesh, in_specs=in_specs, out_specs=out_specs, check_vma=False)
```

```python
import jax
import jax.numpy as jnp
from jax import lax
from jax.experimental import pallas as pl
from jax.experimental.pallas import tpu as pltpu
from jax.sharding import PartitionSpec as P


def coarse_windows(coarse, peers):
    groups, rows, cols = coarse.shape
    tile = rows // peers
    padded = jnp.pad(coarse, ((0, 0), (1, tile - 1), (0, 0)))
    blocks = padded.reshape(groups, peers + 1, tile, cols)
    windows = jnp.concatenate([blocks[:, :peers], blocks[:, 1:, :2]], axis=2)
    windows = jnp.transpose(windows, (1, 2, 0, 3))
    gathered = lax.all_to_all(windows, "row", 0, 0, tiled=True)
    if groups % 8:
        gathered = jnp.transpose(gathered, (1, 0, 2, 3)).reshape(1, tile + 2, peers * groups, cols)
    return gathered


def skip_rows(skip, peers):
    up = [(i, i + 1) for i in range(peers - 1)]
    down = [(j, i) for i, j in up]
    before = lax.ppermute(skip[:, -1:], "row", up)
    after = lax.ppermute(skip[:, :1], "row", down)
    rimmed = jnp.concatenate([before, skip, after], axis=1)
    return jnp.transpose(rimmed, (1, 0, 2))


def lane_shift(v, period, step):
    lane = lax.broadcasted_iota(jnp.int32, v.shape, 1) % period
    edge = 0 if step > 0 else period - 1
    return jnp.where(lane == edge, 0.0, pltpu.roll(v, step % v.shape[1], 1))


def half_weights(w3_ref, first, width):
    cin = w3_ref.shape[1] // 3
    return jnp.concatenate([w3_ref[:, ky * cin + first : ky * cin + first + width] for ky in range(3)], axis=1)


def stacked_rows(field, nout, fw):
    return jnp.concatenate([field[:, ky * fw : (ky + nout) * fw] for ky in range(3)], axis=0)


def combine(total, fw):
    cout = total.shape[0] // 3
    return total[cout : 2 * cout] + lane_shift(total[:cout], fw, 1) + lane_shift(total[2 * cout :], fw, -1)


def skip_kernel(sk_ref, w3_hbm, b3_ref, out_ref, w3_ref, sems):
    cin = w3_hbm.shape[2]
    copies = [pltpu.make_async_copy(w3_hbm.at[ky], w3_ref.at[:, pl.ds(ky * cin, cin)], sems.at[ky]) for ky in range(3)]
    for copy in copies:
        copy.start()
    nfine, skips, fw = sk_ref.shape
    field = jnp.concatenate([sk_ref[t] for t in range(nfine)], axis=1)
    rows = stacked_rows(field, nfine - 2, fw)
    for copy in copies:
        copy.wait()
    total = jnp.dot(half_weights(w3_ref, 0, skips), rows, preferred_element_type=jnp.float32)
    out_ref[...] = combine(total, fw) + b3_ref[...]


def decoder_kernel(flags, xw_ref, part_hbm, wu_hbm, bu_ref, w3_hbm, out_ref, act_ref, part_ref, wu_ref, w3_ref, sems):
    cin = wu_hbm.shape[2]

    def load(src, dst, k):
        copy = pltpu.make_async_copy(src, dst, sems.at[k])
        copy.start()
        return copy

    up_loads = [[load(wu_hbm.at[p + 2 * h], wu_ref.at[p, :, pl.ds(h * cin, cin)], 2 * p + h) for h in range(2)] for p in range(2)]
    conv_loads = [load(w3_hbm.at[ky], w3_ref.at[:, pl.ds(ky * cin, cin)], 4 + ky) for ky in range(3)]
    part_load = load(part_hbm, part_ref, 7)
    peers, nwin, groups, cw = xw_ref.shape
    cout, nout, fw = out_ref.shape
    nfine = nout + 2
    span = (nwin - 1) * cw
    f32 = jnp.float32

    def dot(a, b):
        return jnp.dot(a, b, preferred_element_type=f32)

    def window_row(i):
        if peers == 1:
            return xw_ref[0, i]
        pieces = [xw_ref[s, i].astype(f32) for s in range(peers)]
        return jnp.concatenate(pieces, axis=0).astype(jnp.bfloat16)

    wide = jnp.concatenate([window_row(i) for i in range(nwin)], axis=1)
    stacked = jnp.concatenate([wide[:, cw:], wide[:, :span]], axis=0)
    parity = []
    for p in range(2):
        for copy in up_loads[p]:
            copy.wait()
        z = dot(wu_ref[p], stacked)
        taps = [z[k * cout : (k + 1) * cout] for k in range(4)]
        even = taps[1] + lane_shift(taps[3], cw, 1) + bu_ref[...]
        odd = taps[2] + lane_shift(taps[0], cw, -1) + bu_ref[...]
        parity.append((even.astype(jnp.bfloat16), odd.astype(jnp.bfloat16)))

    col = lax.broadcasted_iota(jnp.int32, (cw, fw), 0)
    pos = lax.broadcasted_iota(jnp.int32, (cw, fw), 1)
    put_even = (pos == 2 * col).astype(jnp.bfloat16)
    put_odd = (pos == 2 * col + 1).astype(jnp.bfloat16)
    put = jnp.concatenate([put_even, put_odd], axis=0)

    joined = []
    for t in range(nfine):
        even, odd = parity[t % 2]
        q = t // 2
        pair = jnp.concatenate([even[:, q * cw : (q + 1) * cw], odd[:, q * cw : (q + 1) * cw]], axis=1)
        row = dot(pair, put)
        if t == 0:
            row = jnp.where(flags[0] == 1, 0.0, row)
        if t == nfine - 1:
            row = jnp.where(flags[1] == 1, 0.0, row)
        joined.append(row.astype(jnp.bfloat16))
    field = jnp.concatenate(joined, axis=1)
    for copy in conv_loads:
        copy.wait()

    skips = w3_ref.shape[1] // 3 - cout
    total = dot(half_weights(w3_ref, skips, cout), stacked_rows(field, nout, fw))
    part_load.wait()
    pre = combine(total, fw) + part_ref[...]
    act = pre / (1.0 + jnp.exp(-pre))
    for y in range(nout):
        act_ref[:, y, :] = act[:, y * fw : (y + 1) * fw]
    out_ref[...] = act_ref[...].astype(out_ref.dtype)


def in_hbm(x):
    return pltpu.with_memory_space_constraint(x, pltpu.HBM)


def decode(flags, xw, part, wu, bu, w3, nfine, fw):
    cout = bu.shape[0]
    vmem = pl.BlockSpec(memory_space=pltpu.VMEM)
    hbm = pl.BlockSpec(memory_space=pltpu.HBM)
    return pl.pallas_call(
        decoder_kernel,
        out_shape=jax.ShapeDtypeStruct((cout, nfine - 2, fw), jnp.bfloat16),
        in_specs=[pl.BlockSpec(memory_space=pltpu.SMEM), vmem, hbm, hbm, vmem, hbm],
        out_specs=vmem,
        scratch_shapes=[
            pltpu.VMEM((cout, nfine - 2, fw), jnp.float32),
            pltpu.VMEM(((cout, (nfine - 2) * fw)), jnp.float32),
            pltpu.VMEM((2, wu.shape[1], 2 * wu.shape[2]), wu.dtype),
            pltpu.VMEM((w3.shape[1], 3 * w3.shape[2]), w3.dtype),
            pltpu.SemaphoreType.DMA((8,)),
        ],
        compiler_params=pltpu.CompilerParams(vmem_limit_bytes=48 * 1024 * 1024),
    )(flags, xw, in_hbm(part), in_hbm(wu), bu, in_hbm(w3))


def skip_conv(sk, w3, b3):
    nfine, cout, fw = sk.shape
    nout = nfine - 2
    vmem = pl.BlockSpec(memory_space=pltpu.VMEM)
    hbm = pl.BlockSpec(memory_space=pltpu.HBM)
    flops = 2 * w3.shape[1] * 3 * cout * nout * fw
    moved = sk.size * 2 + w3.size * 2 + cout * nout * fw * 4
    return pl.pallas_call(
        skip_kernel,
        out_shape=jax.ShapeDtypeStruct((cout, nout * fw), jnp.float32),
        in_specs=[vmem, hbm, vmem],
        out_specs=vmem,
        scratch_shapes=[pltpu.VMEM((w3.shape[1], 3 * w3.shape[2]), w3.dtype), pltpu.SemaphoreType.DMA((3,))],
        compiler_params=pltpu.CompilerParams(vmem_limit_bytes=48 * 1024 * 1024),
        cost_estimate=pl.CostEstimate(flops=flops, transcendentals=0, bytes_accessed=moved),
    )(sk, in_hbm(w3), b3)


def shards(coarse, skip_field, up_weight, up_bias, conv_weight, conv_bias):
    peers = lax.axis_size("row")
    me = lax.axis_index("row")
    flags = jnp.stack([me == 0, me == peers - 1]).astype(jnp.int32)
    sk = skip_rows(skip_field, peers)
    xw = coarse_windows(coarse, peers)
    cout = up_weight.shape[3]
    wu = jnp.transpose(up_weight, (0, 1, 3, 2)).reshape(4, 4 * cout, -1)
    w3 = jnp.transpose(conv_weight, (0, 1, 3, 2)).reshape(3, 3 * cout, -1)
    part = skip_conv(sk, w3, conv_bias[:, None])
    return decode(flags, xw, part, wu, up_bias[:, None], w3, sk.shape[0], sk.shape[2])


def solution(mesh):
    in_specs = (P("row", "member", None), P(None, ("member", "row"), None), P(), P(), P(), P())
    out_specs = P(None, ("member", "row"), None)
    return jax.shard_map(shards, mesh=mesh, in_specs=in_specs, out_specs=out_specs, check_vma=False)
```

```python
import jax
import jax.numpy as jnp
from jax import lax
from jax.experimental import pallas as pl
from jax.experimental.pallas import tpu as pltpu
from jax.sharding import PartitionSpec as P


def coarse_windows(coarse, peers):
    groups, rows, cols = coarse.shape
    tile = rows // peers
    padded = jnp.pad(coarse, ((0, 0), (1, tile - 1), (0, 0)))
    blocks = padded.reshape(groups, peers + 1, tile, cols)
    windows = jnp.concatenate([blocks[:, :peers], blocks[:, 1:, :2]], axis=2)
    windows = jnp.transpose(windows, (1, 2, 0, 3))
    gathered = lax.all_to_all(windows, "row", 0, 0, tiled=True)
    if groups % 8:
        gathered = jnp.transpose(gathered, (1, 0, 2, 3)).reshape(1, tile + 2, peers * groups, cols)
    return gathered


def skip_rows(skip, peers):
    up = [(i, i + 1) for i in range(peers - 1)]
    down = [(j, i) for i, j in up]
    before = lax.ppermute(skip[:, -1:], "row", up)
    after = lax.ppermute(skip[:, :1], "row", down)
    rimmed = jnp.concatenate([before, skip, after], axis=1)
    return jnp.transpose(rimmed, (1, 0, 2))


def lane_shift(v, period, step):
    lane = lax.broadcasted_iota(jnp.int32, v.shape, 1) % period
    edge = 0 if step > 0 else period - 1
    return jnp.where(lane == edge, 0.0, pltpu.roll(v, step % v.shape[1], 1))


def decoder_kernel(flags, xw_ref, sk_ref, wu_hbm, bu_ref, w3_hbm, b3_ref, out_ref, act_ref, wu_ref, w3_ref, sems):
    cin = wu_hbm.shape[2]

    count = []

    def load(src, dst):
        rows = src.shape[0]
        step = rows // 4 if rows % 64 == 0 else rows
        copies = []
        for r0 in range(0, rows, step):
            copy = pltpu.make_async_copy(src.at[pl.ds(r0, step)], dst.at[pl.ds(r0, step)], sems.at[len(count)])
            count.append(r0)
            copy.start()
            copies.append(copy)
        return copies

    up_loads = [sum([load(wu_hbm.at[p + 2 * h], wu_ref.at[p, :, pl.ds(h * cin, cin)]) for h in range(2)], []) for p in range(2)]
    conv_loads = sum([load(w3_hbm.at[ky], w3_ref.at[:, pl.ds(ky * cin, cin)]) for ky in range(3)], [])
    peers, nwin, groups, cw = xw_ref.shape
    nfine, cout, fw = sk_ref.shape
    nout = nfine - 2
    span = (nwin - 1) * cw
    f32 = jnp.float32

    def dot(a, b):
        return jnp.dot(a, b, preferred_element_type=f32)

    def window_row(i):
        if peers == 1:
            return xw_ref[0, i]
        pieces = [xw_ref[s, i].astype(f32) for s in range(peers)]
        return jnp.concatenate(pieces, axis=0).astype(jnp.bfloat16)

    wide = jnp.concatenate([window_row(i) for i in range(nwin)], axis=1)
    stacked = jnp.concatenate([wide[:, cw:], wide[:, :span]], axis=0)
    parity = []
    for p in range(2):
        for copy in up_loads[p]:
            copy.wait()
        z = dot(wu_ref[p], stacked)
        taps = [z[k * cout : (k + 1) * cout] for k in range(4)]
        even = taps[1] + lane_shift(taps[3], cw, 1) + bu_ref[...]
        odd = taps[2] + lane_shift(taps[0], cw, -1) + bu_ref[...]
        parity.append((even.astype(jnp.bfloat16), odd.astype(jnp.bfloat16)))

    col = lax.broadcasted_iota(jnp.int32, (cw, fw), 0)
    pos = lax.broadcasted_iota(jnp.int32, (cw, fw), 1)
    put_even = (pos == 2 * col).astype(jnp.bfloat16)
    put_odd = (pos == 2 * col + 1).astype(jnp.bfloat16)
    put = jnp.concatenate([put_even, put_odd], axis=0)

    joined = []
    for t in range(nfine):
        even, odd = parity[t % 2]
        q = t // 2
        pair = jnp.concatenate([even[:, q * cw : (q + 1) * cw], odd[:, q * cw : (q + 1) * cw]], axis=1)
        row = dot(pair, put)
        if t == 0:
            row = jnp.where(flags[0] == 1, 0.0, row)
        if t == nfine - 1:
            row = jnp.where(flags[1] == 1, 0.0, row)
        joined.append(jnp.concatenate([sk_ref[t], row.astype(jnp.bfloat16)], axis=0))
    field = jnp.concatenate(joined, axis=1)
    for copy in conv_loads:
        copy.wait()

    rows = jnp.concatenate([field[:, ky * fw : (ky + nout) * fw] for ky in range(3)], axis=0)
    total = dot(w3_ref[...], rows)
    pre = total[cout : 2 * cout]
    pre = pre + lane_shift(total[:cout], fw, 1) + lane_shift(total[2 * cout :], fw, -1)
    pre = pre + b3_ref[...]
    act = pre / (1.0 + jnp.exp(-pre))
    for y in range(nout):
        act_ref[:, y, :] = act[:, y * fw : (y + 1) * fw]
    out_ref[...] = act_ref[...].astype(out_ref.dtype)


def decode(flags, xw, sk, wu, bu, w3, b3):
    nfine, cout, fw = sk.shape
    vmem = pl.BlockSpec(memory_space=pltpu.VMEM)
    hbm = pl.BlockSpec(memory_space=pltpu.HBM)
    return pl.pallas_call(
        decoder_kernel,
        out_shape=jax.ShapeDtypeStruct((cout, nfine - 2, fw), jnp.bfloat16),
        in_specs=[pl.BlockSpec(memory_space=pltpu.SMEM), vmem, vmem, hbm, vmem, hbm, vmem],
        out_specs=vmem,
        scratch_shapes=[
            pltpu.VMEM((cout, nfine - 2, fw), jnp.float32),
            pltpu.VMEM((2, wu.shape[1], 2 * wu.shape[2]), wu.dtype),
            pltpu.VMEM((w3.shape[1], 3 * w3.shape[2]), w3.dtype),
            pltpu.SemaphoreType.DMA((28,)),
        ],
        compiler_params=pltpu.CompilerParams(vmem_limit_bytes=48 * 1024 * 1024),
    )(flags, xw, sk, pltpu.with_memory_space_constraint(wu, pltpu.HBM), bu, pltpu.with_memory_space_constraint(w3, pltpu.HBM), b3)


def shards(coarse, skip_field, up_weight, up_bias, conv_weight, conv_bias):
    peers = lax.axis_size("row")
    me = lax.axis_index("row")
    flags = jnp.stack([me == 0, me == peers - 1]).astype(jnp.int32)
    sk = skip_rows(skip_field, peers)
    xw = coarse_windows(coarse, peers)
    cout = up_weight.shape[3]
    wu = jnp.transpose(up_weight, (0, 1, 3, 2)).reshape(4, 4 * cout, -1)
    w3 = jnp.transpose(conv_weight, (0, 1, 3, 2)).reshape(3, 3 * cout, -1)
    return decode(flags, xw, sk, wu, up_bias[:, None], w3, conv_bias[:, None])


def solution(mesh):
    in_specs = (P("row", "member", None), P(None, ("member", "row"), None), P(), P(), P(), P())
    out_specs = P(None, ("member", "row"), None)
    return jax.shard_map(shards, mesh=mesh, in_specs=in_specs, out_specs=out_specs, check_vma=False)
```

```python
import jax
import jax.numpy as jnp
from jax import lax
from jax.experimental import pallas as pl
from jax.experimental.pallas import tpu as pltpu
from jax.sharding import PartitionSpec as P


def coarse_windows(coarse, peers):
    groups, rows, cols = coarse.shape
    tile = rows // peers
    padded = jnp.pad(coarse, ((0, 0), (1, tile - 1), (0, 0)))
    blocks = padded.reshape(groups, peers + 1, tile, cols)
    windows = jnp.concatenate([blocks[:, :peers], blocks[:, 1:, :2]], axis=2)
    windows = jnp.transpose(windows, (1, 2, 0, 3))
    gathered = lax.all_to_all(windows, "row", 0, 0, tiled=True)
    if groups % 8:
        gathered = jnp.transpose(gathered, (1, 0, 2, 3)).reshape(1, tile + 2, peers * groups, cols)
    return gathered


def skip_rows(skip, peers):
    up = [(i, i + 1) for i in range(peers - 1)]
    down = [(j, i) for i, j in up]
    before = lax.ppermute(skip[:, -1:], "row", up)
    after = lax.ppermute(skip[:, :1], "row", down)
    rimmed = jnp.concatenate([before, skip, after], axis=1)
    return jnp.transpose(rimmed, (1, 0, 2))


def lane_shift(v, period, step):
    lane = lax.broadcasted_iota(jnp.int32, v.shape, 1) % period
    edge = 0 if step > 0 else period - 1
    return jnp.where(lane == edge, 0.0, pltpu.roll(v, step % v.shape[1], 1))


def decoder_kernel(flags, xw_ref, sk_ref, wu_hbm, bu_ref, w3_hbm, b3_ref, out_ref, act_ref, wu_ref, w3_ref, sems):
    cin = wu_hbm.shape[2]

    def load(src, dst, k):
        copy = pltpu.make_async_copy(src, dst, sems.at[k])
        copy.start()
        return copy

    up_loads = [[load(wu_hbm.at[p + 2 * h], wu_ref.at[p, :, pl.ds(h * cin, cin)], 2 * p + h) for h in range(2)] for p in range(2)]
    conv_loads = [load(w3_hbm.at[ky], w3_ref.at[:, pl.ds(ky * cin, cin)], 4 + ky) for ky in range(3)]
    peers, nwin, groups, cw = xw_ref.shape
    nfine, cout, fw = sk_ref.shape
    nout = nfine - 2
    span = (nwin - 1) * cw
    f32 = jnp.float32

    def dot(a, b):
        return jnp.dot(a, b, preferred_element_type=f32)

    def window_row(i):
        if peers == 1:
            return xw_ref[0, i]
        return jnp.concatenate([xw_ref[s, i] for s in range(peers)], axis=0)

    wide = jnp.concatenate([window_row(i) for i in range(nwin)], axis=1)
    stacked = jnp.concatenate([wide[:, cw:], wide[:, :span]], axis=0)
    parity = []
    for p in range(2):
        for copy in up_loads[p]:
            copy.wait()
        z = dot(wu_ref[p], stacked)
        taps = [z[k * cout : (k + 1) * cout] for k in range(4)]
        even = taps[1] + lane_shift(taps[3], cw, 1) + bu_ref[...]
        odd = taps[2] + lane_shift(taps[0], cw, -1) + bu_ref[...]
        parity.append((even.astype(jnp.bfloat16), odd.astype(jnp.bfloat16)))

    col = lax.broadcasted_iota(jnp.int32, (cw, fw), 0)
    pos = lax.broadcasted_iota(jnp.int32, (cw, fw), 1)
    put_even = (pos == 2 * col).astype(jnp.bfloat16)
    put_odd = (pos == 2 * col + 1).astype(jnp.bfloat16)
    put = jnp.concatenate([put_even, put_odd], axis=0)

    joined = []
    for t in range(nfine):
        even, odd = parity[t % 2]
        q = t // 2
        pair = jnp.concatenate([even[:, q * cw : (q + 1) * cw], odd[:, q * cw : (q + 1) * cw]], axis=1)
        row = dot(pair, put)
        if t == 0:
            row = jnp.where(flags[0] == 1, 0.0, row)
        if t == nfine - 1:
            row = jnp.where(flags[1] == 1, 0.0, row)
        joined.append(jnp.concatenate([sk_ref[t], row.astype(jnp.bfloat16)], axis=0))
    field = jnp.concatenate(joined, axis=1)
    for copy in conv_loads:
        copy.wait()

    rows = jnp.concatenate([field[:, ky * fw : (ky + nout) * fw] for ky in range(3)], axis=0)
    total = dot(w3_ref[...], rows)
    pre = total[cout : 2 * cout]
    pre = pre + lane_shift(total[:cout], fw, 1) + lane_shift(total[2 * cout :], fw, -1)
    pre = pre + b3_ref[...]
    act = pre / (1.0 + jnp.exp(-pre))
    for y in range(nout):
        act_ref[:, y, :] = act[:, y * fw : (y + 1) * fw]
    out_ref[...] = act_ref[...].astype(out_ref.dtype)


def decode(flags, xw, sk, wu, bu, w3, b3):
    nfine, cout, fw = sk.shape
    vmem = pl.BlockSpec(memory_space=pltpu.VMEM)
    hbm = pl.BlockSpec(memory_space=pltpu.HBM)
    return pl.pallas_call(
        decoder_kernel,
        out_shape=jax.ShapeDtypeStruct((cout, nfine - 2, fw), jnp.bfloat16),
        in_specs=[pl.BlockSpec(memory_space=pltpu.SMEM), vmem, vmem, hbm, vmem, hbm, vmem],
        out_specs=vmem,
        scratch_shapes=[
            pltpu.VMEM((cout, nfine - 2, fw), jnp.float32),
            pltpu.VMEM((2, wu.shape[1], 2 * wu.shape[2]), wu.dtype),
            pltpu.VMEM((w3.shape[1], 3 * w3.shape[2]), w3.dtype),
            pltpu.SemaphoreType.DMA((7,)),
        ],
        compiler_params=pltpu.CompilerParams(vmem_limit_bytes=48 * 1024 * 1024),
    )(flags, xw, sk, pltpu.with_memory_space_constraint(wu, pltpu.HBM), bu, pltpu.with_memory_space_constraint(w3, pltpu.HBM), b3)


def shards(coarse, skip_field, up_weight, up_bias, conv_weight, conv_bias):
    peers = lax.axis_size("row")
    me = lax.axis_index("row")
    flags = jnp.stack([me == 0, me == peers - 1]).astype(jnp.int32)
    sk = skip_rows(skip_field, peers)
    xw = coarse_windows(coarse, peers)
    cout = up_weight.shape[3]
    wu = jnp.transpose(up_weight, (0, 1, 3, 2)).reshape(4, 4 * cout, -1)
    w3 = jnp.transpose(conv_weight, (0, 1, 3, 2)).reshape(3, 3 * cout, -1)
    return decode(flags, xw, sk, wu, up_bias[:, None], w3, conv_bias[:, None])


def solution(mesh):
    in_specs = (P("row", "member", None), P(None, ("member", "row"), None), P(), P(), P(), P())
    out_specs = P(None, ("member", "row"), None)
    return jax.shard_map(shards, mesh=mesh, in_specs=in_specs, out_specs=out_specs, check_vma=False)
```

```python
import jax
import jax.numpy as jnp
from jax import lax
from jax.experimental import pallas as pl
from jax.experimental.pallas import tpu as pltpu
from jax.sharding import PartitionSpec as P


def coarse_windows(coarse, peers):
    groups, rows, cols = coarse.shape
    tile = rows // peers
    padded = jnp.pad(coarse, ((0, 0), (1, tile - 1), (0, 0)))
    blocks = padded.reshape(groups, peers + 1, tile, cols)
    windows = jnp.concatenate([blocks[:, :peers], blocks[:, 1:, :2]], axis=2)
    windows = jnp.transpose(windows, (1, 2, 0, 3))
    gathered = lax.all_to_all(windows, "row", 0, 0, tiled=True)
    if groups % 8:
        gathered = jnp.transpose(gathered, (1, 0, 2, 3)).reshape(1, tile + 2, peers * groups, cols)
    return gathered


def skip_rows(skip, peers):
    up = [(i, i + 1) for i in range(peers - 1)]
    down = [(j, i) for i, j in up]
    before = lax.ppermute(skip[:, -1:], "row", up)
    after = lax.ppermute(skip[:, :1], "row", down)
    rimmed = jnp.concatenate([before, skip, after], axis=1)
    return jnp.transpose(rimmed, (1, 0, 2))


def lane_shift(v, period, step):
    lane = lax.broadcasted_iota(jnp.int32, v.shape, 1) % period
    edge = 0 if step > 0 else period - 1
    return jnp.where(lane == edge, 0.0, pltpu.roll(v, step % v.shape[1], 1))


def decoder_kernel(flags, xw_ref, sk_ref, wu_hbm, bu_ref, w3_hbm, b3_ref, out_ref, act_ref, wu_ref, w3_ref, sems):
    cin = wu_hbm.shape[2]

    def load(src, dst, k):
        copy = pltpu.make_async_copy(src, dst, sems.at[k])
        copy.start()
        return copy

    up_loads = [[load(wu_hbm.at[p + 2 * h], wu_ref.at[p, :, pl.ds(h * cin, cin)], 2 * p + h) for h in range(2)] for p in range(2)]
    conv_loads = [load(w3_hbm.at[ky], w3_ref.at[:, pl.ds(ky * cin, cin)], 4 + ky) for ky in range(3)]
    peers, nwin, groups, cw = xw_ref.shape
    nfine, cout, fw = sk_ref.shape
    nout = nfine - 2
    span = (nwin - 1) * cw
    f32 = jnp.float32

    def dot(a, b):
        return jnp.dot(a, b, preferred_element_type=f32)

    def window_row(i):
        if peers == 1:
            return xw_ref[0, i]
        pieces = [xw_ref[s, i].astype(f32) for s in range(peers)]
        return jnp.concatenate(pieces, axis=0).astype(jnp.bfloat16)

    wide = jnp.concatenate([window_row(i) for i in range(nwin)], axis=1)
    stacked = jnp.concatenate([wide[:, cw:], wide[:, :span]], axis=0)
    parity = []
    for p in range(2):
        for copy in up_loads[p]:
            copy.wait()
        z = dot(wu_ref[p], stacked)
        taps = [z[k * cout : (k + 1) * cout] for k in range(4)]
        even = taps[1] + lane_shift(taps[3], cw, 1) + bu_ref[...]
        odd = taps[2] + lane_shift(taps[0], cw, -1) + bu_ref[...]
        parity.append((even.astype(jnp.bfloat16), odd.astype(jnp.bfloat16)))

    col = lax.broadcasted_iota(jnp.int32, (cw, fw), 0)
    pos = lax.broadcasted_iota(jnp.int32, (cw, fw), 1)
    put_even = (pos == 2 * col).astype(jnp.bfloat16)
    put_odd = (pos == 2 * col + 1).astype(jnp.bfloat16)
    put = jnp.concatenate([put_even, put_odd], axis=0)

    joined = []
    for t in range(nfine):
        even, odd = parity[t % 2]
        q = t // 2
        pair = jnp.concatenate([even[:, q * cw : (q + 1) * cw], odd[:, q * cw : (q + 1) * cw]], axis=1)
        row = dot(pair, put)
        if t == 0:
            row = jnp.where(flags[0] == 1, 0.0, row)
        if t == nfine - 1:
            row = jnp.where(flags[1] == 1, 0.0, row)
        joined.append(jnp.concatenate([sk_ref[t], row.astype(jnp.bfloat16)], axis=0))
    field = jnp.concatenate(joined, axis=1)
    for copy in conv_loads:
        copy.wait()

    rows = jnp.concatenate([field[:, ky * fw : (ky + nout) * fw] for ky in range(3)], axis=0)
    total = dot(w3_ref[...], rows)
    pre = total[cout : 2 * cout]
    pre = pre + lane_shift(total[:cout], fw, 1) + lane_shift(total[2 * cout :], fw, -1)
    pre = pre + b3_ref[...]
    act = pre * jax.nn.sigmoid(pre)
    for y in range(nout):
        act_ref[:, y, :] = act[:, y * fw : (y + 1) * fw]
    out_ref[...] = act_ref[...].astype(out_ref.dtype)


def decode(flags, xw, sk, wu, bu, w3, b3):
    nfine, cout, fw = sk.shape
    vmem = pl.BlockSpec(memory_space=pltpu.VMEM)
    hbm = pl.BlockSpec(memory_space=pltpu.HBM)
    return pl.pallas_call(
        decoder_kernel,
        out_shape=jax.ShapeDtypeStruct((cout, nfine - 2, fw), jnp.bfloat16),
        in_specs=[pl.BlockSpec(memory_space=pltpu.SMEM), vmem, vmem, hbm, vmem, hbm, vmem],
        out_specs=vmem,
        scratch_shapes=[
            pltpu.VMEM((cout, nfine - 2, fw), jnp.float32),
            pltpu.VMEM((2, wu.shape[1], 2 * wu.shape[2]), wu.dtype),
            pltpu.VMEM((w3.shape[1], 3 * w3.shape[2]), w3.dtype),
            pltpu.SemaphoreType.DMA((7,)),
        ],
        compiler_params=pltpu.CompilerParams(vmem_limit_bytes=48 * 1024 * 1024),
    )(flags, xw, sk, pltpu.with_memory_space_constraint(wu, pltpu.HBM), bu, pltpu.with_memory_space_constraint(w3, pltpu.HBM), b3)


def shards(coarse, skip_field, up_weight, up_bias, conv_weight, conv_bias):
    peers = lax.axis_size("row")
    me = lax.axis_index("row")
    flags = jnp.stack([me == 0, me == peers - 1]).astype(jnp.int32)
    sk = skip_rows(skip_field, peers)
    xw = coarse_windows(coarse, peers)
    cout = up_weight.shape[3]
    wu = jnp.transpose(up_weight, (0, 1, 3, 2)).reshape(4, 4 * cout, -1)
    w3 = jnp.transpose(conv_weight, (0, 1, 3, 2)).reshape(3, 3 * cout, -1)
    return decode(flags, xw, sk, wu, up_bias[:, None], w3, conv_bias[:, None])


def solution(mesh):
    in_specs = (P("row", "member", None), P(None, ("member", "row"), None), P(), P(), P(), P())
    out_specs = P(None, ("member", "row"), None)
    return jax.shard_map(shards, mesh=mesh, in_specs=in_specs, out_specs=out_specs, check_vma=False)
```
